128 devices in a mesh: ctx: 16 (over z, y_hi, core), tp: 8 (over x, y_lo).
Axes of the slice: x: 4, y: 4 (y_hi: 2, y_lo: 2; y = y_hi * 2 + y_lo), z: 4, core: 2. Of those that a mesh axis runs over, the one named last changes fastest.
Arguments:
- queries: bfloat16 [16384, 2048], P('ctx', 'tp'), may hold values from -8 to 8
- keys: bfloat16 [16384, 2048], P('ctx', 'tp'), may hold values from -8 to 8
- values: bfloat16 [16384, 2048], P('ctx', 'tp'), may hold values from -6 to 6
- out_weight: bfloat16 [2048, 4096], P('tp'), may hold values from -0.125 to 0.125
- cotangent: bfloat16 [16384, 4096], P('ctx', 'tp'), may hold values from -6 to 6
- block_keep: int32 [16, 16], replicated, may hold values 0 or 1
Outputs:
- mixed: bfloat16 [16384, 4096], P('ctx', 'tp')
- d_queries: float32 [16384, 2048], P('ctx', 'tp')
- d_keys: float32 [16384, 2048], P('ctx', 'tp')
- d_values: float32 [16384, 2048], P('ctx', 'tp')
- d_weight: float32 [2048, 4096], P('tp', 'ctx')
The draws below stay inside these ranges and needn't reach their ends.
All inputs are finite; a program needn't handle non-finite values.
Results may differ from the reference program's by a relative error of at most 0.014.
Values may be sent and summed in bfloat16 or wider, within the bound.
No kernel may reach another device: no remote copies, remote signals or barrier semaphores. Data moves between devices by JAX's collectives and lax.ppermute only.
A program may use at most 192 MiB of HBM per device.

```python
import math
import jax
import jax.numpy as jnp
from jax import lax

D = 4096
HEADS = 16
DH = 128
BLOCK = 1024
HD = 2048
LEVELS = 4
SEQ = 16384
N_CTX = 16


def row_scales(key, lower, upper):
    return jnp.exp(jax.random.uniform(key, (SEQ, 1), jnp.float32, math.log(lower), math.log(upper)))


def draw_queries(key, part):
    base = jax.random.normal(jax.random.fold_in(key, 21), (SEQ, HD), jnp.float32)
    base = base * row_scales(jax.random.fold_in(key, 22), 0.3, 1.5)
    base = jnp.clip(base, -8.0, 8.0)
    return base.astype(jnp.bfloat16)


def draw_keys(key, part):
    base = jax.random.normal(jax.random.fold_in(key, 31), (SEQ, HD), jnp.float32)
    base = base * row_scales(jax.random.fold_in(key, 32), 0.25, 2.5)
    base = jnp.clip(base, -8.0, 8.0)
    return base.astype(jnp.bfloat16)


def touch_ends(entries, rng, low, high):
    shape = entries.shape
    place = [jax.random.randint(jax.random.fold_in(rng, axis), (), 0, shape[axis]) for axis in range(len(shape))]
    entries = entries.at[tuple(place)].set(low)
    longest = shape.index(max(shape))
    place[longest] = (place[longest] + 1) % shape[longest]
    return entries.at[tuple(place)].set(high)


def with_spikes(entries, own_key, source, target, parts, factor):
    owner, partner = [(jnp.arange(entries.shape[dim]) // (entries.shape[dim] // parts)).reshape([-1 if axis == dim else 1 for axis in range(entries.ndim)]) for dim in (source, target)]
    chosen = jax.random.permutation(own_key, parts)[partner]
    strong = (owner == chosen) | (owner == (partner + parts // 2) % parts)
    return jnp.where(strong, factor * entries, entries)


def levels(own_key, extent, split, smallest, top_value):
    def one(dim, blocks):
        heights = jax.random.uniform(jax.random.fold_in(jax.random.fold_in(own_key, 6), dim), (blocks,), jnp.float32, smallest / len(split), top_value / len(split))
        return jnp.repeat(jnp.exp(heights), extent[dim] // blocks).reshape((-1,) + (1,) * (len(extent) - dim - 1))

    level = one(*split[0])
    for cut in split[1:]:
        level = level * one(*cut)
    return level


def bell_draw(own_key, dims, scale, most, split=(), kind=jnp.bfloat16):
    loudness = levels(own_key, dims, split, -0.22, 0.18) if split else 1.0
    drawn = jax.random.normal(own_key, dims, jnp.float32) * scale * loudness
    return jnp.minimum(jnp.maximum(drawn, -most), most).astype(kind)


def gaussian_with(stream_key, extent, deviation, limit, split, heavy, held_as=jnp.bfloat16):
    result = deviation * jax.random.normal(stream_key, extent, jnp.float32)
    if split:
        result = result * levels(stream_key, extent, split, -0.22, 0.18)
    return jnp.clip(with_spikes(result, jax.random.fold_in(stream_key, 3), *heavy), -limit, limit).astype(held_as)


def setup_inputs(seed: int = 0) -> dict:
    key_list = jax.random.split(jax.random.key(seed), 7)
    queries = draw_queries(jax.random.fold_in(key_list[6], 71), 0)
    keys = draw_keys(jax.random.fold_in(key_list[6], 71), 0)
    values = bell_draw(key_list[2], (SEQ, HD), 1.0, 6.0, ((0, 16), (1, 8)))
    out_weight = bell_draw(key_list[3], (HD, D), HD ** -0.5, 0.125, ((0, 8),))
    cotangent = gaussian_with(key_list[4], (SEQ, D), 1.0, 6.0, ((0, 16), (1, 8)), (0, 1, 16, 2.0))
    block_keep = touch_ends((jax.random.randint(key_list[5], (N_CTX, N_CTX), 0, 4) < 3).astype(jnp.int32), jax.random.fold_in(key_list[5], 1), 0, 1)
    return dict(queries=queries, keys=keys, values=values, out_weight=out_weight, cotangent=cotangent, block_keep=block_keep)


NEG = -1e+30

def reference(queries, keys, values, out_weight, cotangent, block_keep):
    score_scale = 1.0 / math.sqrt(DH)
    block_count = SEQ // BLOCK
    query_heads = queries.reshape(SEQ, HEADS, DH).astype(jnp.float32)
    key_heads = keys.reshape(SEQ, HEADS, DH).astype(jnp.float32)
    value_heads = values.reshape(SEQ, HEADS, DH).astype(jnp.float32)
    grad_full = jnp.dot(cotangent, out_weight.T, preferred_element_type=jnp.float32)
    grad_rounded = lax.optimization_barrier(grad_full.astype(jnp.bfloat16))
    grad_heads = grad_rounded.astype(jnp.float32).reshape(SEQ, HEADS, DH)
    rows_ids = jnp.arange(BLOCK, dtype=jnp.int32)
    causal = rows_ids[:, None] >= rows_ids[None, :]
    attended_parts = []
    query_grads = []
    grad_key = jnp.zeros((SEQ, HEADS, DH), jnp.float32)
    grad_value = jnp.zeros((SEQ, HEADS, DH), jnp.float32)
    for block in range(block_count):
        sources = [block] + [block - 2 ** level for level in range(LEVELS) if 2 ** level <= block]
        low = block * BLOCK
        query_block = query_heads[low:low + BLOCK]
        grad_block = grad_heads[low:low + BLOCK]
        key_cat = jnp.concatenate([key_heads[s * BLOCK:(s + 1) * BLOCK] for s in sources], axis=0)
        value_cat = jnp.concatenate([value_heads[s * BLOCK:(s + 1) * BLOCK] for s in sources], axis=0)
        allow_parts = [causal] + [jnp.broadcast_to(block_keep[block, s] == 1, (BLOCK, BLOCK)) for s in sources[1:]]
        allow = jnp.concatenate(allow_parts, axis=1)
        scores = jnp.einsum('thd,uhd->htu', query_block, key_cat) * score_scale
        masked = jnp.where(allow[None], scores, NEG)
        top = lax.optimization_barrier(jnp.max(masked, axis=2, keepdims=True))
        expd = jnp.exp(masked - top)
        probs = expd / lax.optimization_barrier(jnp.sum(expd, axis=2, keepdims=True))
        rounded = lax.optimization_barrier(probs.astype(jnp.bfloat16)).astype(jnp.float32)
        attended32 = jnp.einsum('htu,uhd->thd', rounded, value_cat)
        attended_parts.append(attended32)
        dots = jnp.einsum('thd,uhd->htu', grad_block, value_cat)
        delta = jnp.transpose(lax.optimization_barrier(jnp.sum(grad_block * attended32, axis=2)))[:, :, None]
        slopes = probs * (dots - delta) * score_scale
        slopes = lax.optimization_barrier(slopes.astype(jnp.bfloat16)).astype(jnp.float32)
        query_grads.append(jnp.einsum('htu,uhd->thd', slopes, key_cat))
        key_part = jnp.einsum('htu,thd->uhd', slopes, query_block)
        value_part = jnp.einsum('htu,thd->uhd', rounded, grad_block)
        for number, s in enumerate(sources):
            grad_key = grad_key.at[s * BLOCK:(s + 1) * BLOCK].add(key_part[number * BLOCK:(number + 1) * BLOCK])
            grad_value = grad_value.at[s * BLOCK:(s + 1) * BLOCK].add(value_part[number * BLOCK:(number + 1) * BLOCK])
    attended = jnp.concatenate(attended_parts, axis=0).reshape(SEQ, HD).astype(jnp.bfloat16)
    mixed = jnp.dot(attended, out_weight, preferred_element_type=jnp.float32).astype(jnp.bfloat16)
    d_weight = jnp.dot(attended.T, cotangent, preferred_element_type=jnp.float32)
    d_queries = jnp.concatenate(query_grads, axis=0).reshape(SEQ, HD)
    return (mixed, d_queries, grad_key.reshape(SEQ, HD), grad_value.reshape(SEQ, HD), d_weight)
```

```python
import math

import jax
import jax.numpy as jnp
from jax import lax
from jax.sharding import PartitionSpec as P

DH = 128


NEG = -1e30


def passed_along(value, axis, steps):
    count = lax.axis_size(axis)
    initial, last = (max(0, -steps), min(count, count - steps))
    return lax.ppermute(value, axis, [(source, source + steps) for source in range(initial, last)])


def gathered(piece, axis):
    count = lax.axis_size(axis)
    spread = jnp.broadcast_to(piece[None], (count,) + piece.shape)
    parts = lax.all_to_all(spread, axis, 0, 0, tiled=True)
    return jnp.moveaxis(parts, 0, 1).reshape(piece.shape[0], count * piece.shape[1])


def summed_scatter(part, axis):
    count = lax.axis_size(axis)
    rows, cols = part.shape
    pieces = part.reshape(rows, count, cols // count)
    parts = lax.all_to_all(pieces, axis, 1, 1, tiled=True)
    return jnp.sum(parts.astype(jnp.float32), axis=1)


def local(queries, keys, values, out_weight, cotangent, block_keep):
    block_len = queries.shape[0]
    local_cols = queries.shape[1]
    local_heads = local_cols // DH
    score_scale = 1.0 / math.sqrt(DH)
    axis_len = lax.axis_size("ctx")
    levels = axis_len.bit_length() - 1
    block_index = lax.axis_index("ctx")
    query_heads = queries.reshape(block_len, local_heads, DH)
    stacked = jnp.stack([keys, values])
    remote = [passed_along(stacked, "ctx", 1 << level) for level in range(levels)]
    blocks = [stacked] + remote
    row_pick = lax.broadcasted_iota(jnp.int32, block_keep.shape, 0) == block_index
    keep_row = jnp.sum(jnp.where(row_pick, block_keep, 0), axis=0)
    column_ids = lax.broadcasted_iota(jnp.int32, keep_row.shape, 0)
    flags = []
    for level in range(levels):
        target = block_index - (1 << level)
        linked = jnp.sum(jnp.where(column_ids == target, keep_row, 0))
        flags.append((target >= 0) & (linked == 1))
    causal = lax.broadcasted_iota(jnp.int32, (block_len, block_len), 0) >= lax.broadcasted_iota(
        jnp.int32, (block_len, block_len), 1
    )

    def heads_of(number, which):
        return blocks[number][which].reshape(block_len, local_heads, DH)

    def scores_for(number):
        raw = (
            jnp.einsum(
                "thd,uhd->htu", query_heads, heads_of(number, 0), preferred_element_type=jnp.float32
            )
            * score_scale
        )
        if number == 0:
            return jnp.where(causal[None], raw, NEG)
        return jnp.where(flags[number - 1], raw, NEG)

    running_max = jnp.full((local_heads, block_len, 1), NEG, jnp.float32)
    running_total = jnp.zeros((local_heads, block_len, 1), jnp.float32)
    for number in range(len(blocks)):
        scores = scores_for(number)
        new_max = jnp.maximum(running_max, jnp.max(scores, axis=2, keepdims=True))
        running_total = running_total * jnp.exp(running_max - new_max) + jnp.sum(
            jnp.exp(scores - new_max), axis=2, keepdims=True
        )
        running_max = new_max
    attended32 = jnp.zeros((block_len, local_heads, DH), jnp.float32)
    for number in range(len(blocks)):
        probs = jnp.exp(scores_for(number) - running_max) / running_total
        weights = probs.astype(jnp.bfloat16)
        attended32 = attended32 + jnp.einsum(
            "htu,uhd->thd", weights, heads_of(number, 1), preferred_element_type=jnp.float32
        )
    attended = attended32.reshape(block_len, local_cols).astype(jnp.bfloat16)
    weight_cols = lax.all_to_all(out_weight, "tp", split_axis=1, concat_axis=0, tiled=True)
    mixed_sum = jnp.dot(
        gathered(attended, "tp"),
        weight_cols,
        preferred_element_type=jnp.float32,
    )
    mixed = mixed_sum.astype(jnp.bfloat16)
    piece = gathered(cotangent, "tp")
    grad_att = lax.dot_general(
        piece, out_weight, (((1,), (1,)), ((), ())), preferred_element_type=jnp.float32
    )
    weight_part = lax.dot_general(
        attended, piece, (((0,), (0,)), ((), ())), preferred_element_type=jnp.float32
    )
    grad_weight = weight_part
    grad_att, grad_weight = (grad_att, grad_weight)
    d_weight = summed_scatter(grad_weight.astype(jnp.bfloat16), "ctx")
    grad_heads = grad_att.reshape(block_len, local_heads, DH).astype(jnp.bfloat16)
    delta = jnp.transpose(jnp.sum(grad_heads.astype(jnp.float32) * attended32, axis=2))[:, :, None]
    grad_query = jnp.zeros((block_len, local_heads, DH), jnp.float32)
    returns = []
    for number in range(len(blocks)):
        probs = jnp.exp(scores_for(number) - running_max) / running_total
        weights = probs.astype(jnp.bfloat16)
        dots = jnp.einsum(
            "thd,uhd->htu", grad_heads, heads_of(number, 1), preferred_element_type=jnp.float32
        )
        slopes = (probs * (dots - delta) * score_scale).astype(jnp.bfloat16)
        grad_query = grad_query + jnp.einsum(
            "htu,uhd->thd", slopes, heads_of(number, 0), preferred_element_type=jnp.float32
        )
        grad_key = jnp.einsum(
            "htu,thd->uhd", slopes, query_heads, preferred_element_type=jnp.float32
        )
        grad_value = jnp.einsum(
            "htu,thd->uhd", weights, grad_heads, preferred_element_type=jnp.float32
        )
        returns.append(
            jnp.stack(
                [grad_key.reshape(block_len, local_cols), grad_value.reshape(block_len, local_cols)]
            )
        )
    own_grads = returns[0]
    for level in range(levels):
        arrived = passed_along(
            returns[level + 1].astype(jnp.bfloat16), "ctx", -(1 << level)
        ).astype(jnp.float32)
        own_grads = own_grads + arrived
    return (mixed, grad_query.reshape(block_len, local_cols), own_grads[0], own_grads[1], d_weight)


def solution(mesh):
    in_specs = (P("ctx", "tp"), P("ctx", "tp"), P("ctx", "tp"), P("tp", None), P("ctx", "tp"), P())
    out_specs = (P("ctx", "tp"), P("ctx", "tp"), P("ctx", "tp"), P("ctx", "tp"), P("tp", "ctx"))
    return jax.shard_map(local, mesh=mesh, in_specs=in_specs, out_specs=out_specs, check_vma=False)
```

```python
import functools
import math

import jax
import jax.numpy as jnp
from jax import lax
from jax.experimental import pallas as pl
from jax.experimental.pallas import tpu as pltpu
from jax.sharding import PartitionSpec as P

DH = 128
NEG = -1e30
KEY_TILE = 512


def passed_along(value, axis, steps):
    count = lax.axis_size(axis)
    initial, last = (max(0, -steps), min(count, count - steps))
    return lax.ppermute(value, axis, [(source, source + steps) for source in range(initial, last)])


def gathered(piece, axis):
    count = lax.axis_size(axis)
    spread = jnp.broadcast_to(piece[None], (count,) + piece.shape)
    parts = lax.all_to_all(spread, axis, 0, 0, tiled=True)
    return jnp.moveaxis(parts, 0, 1).reshape(piece.shape[0], count * piece.shape[1])


def summed_scatter(part, axis):
    count = lax.axis_size(axis)
    rows, cols = part.shape
    pieces = part.reshape(rows, count, cols // count)
    parts = lax.all_to_all(pieces, axis, 1, 1, tiled=True)
    return jnp.sum(parts.astype(jnp.float32), axis=1)


def masked_scores(flag_ref, q, k, step, tiles, scale):
    block = step // tiles
    tile = step % tiles
    raw = lax.dot_general(q, k, (((1,), (1,)), ((), ())), preferred_element_type=jnp.float32) * scale
    rows = lax.broadcasted_iota(jnp.int32, raw.shape, 0)
    cols = lax.broadcasted_iota(jnp.int32, raw.shape, 1) + tile * raw.shape[1]
    reach = 1 << 20
    offset = jnp.where(block == 0, 0, jnp.where(flag_ref[block] == 1, reach, -reach))
    return jnp.where(rows + offset >= cols, raw, NEG)


def forward_kernel(flag_ref, q_ref, k_ref, v_ref, att_ref, m_ref, l_ref, m_sc, l_sc, acc_sc, *, tiles, steps, scale):
    phase = pl.program_id(1)
    step = pl.program_id(2)
    scores = masked_scores(flag_ref, q_ref[...], k_ref[...], step, tiles, scale)

    @pl.when((phase == 0) & (step == 0))
    def _():
        m_sc[...] = jnp.full(m_sc.shape, NEG, jnp.float32)
        l_sc[...] = jnp.zeros(l_sc.shape, jnp.float32)

    @pl.when(phase == 0)
    def _():
        old = m_sc[...]
        new = jnp.maximum(old, jnp.max(scores, axis=1, keepdims=True))
        l_sc[...] = l_sc[...] * jnp.exp(old - new) + jnp.sum(jnp.exp(scores - new), axis=1, keepdims=True)
        m_sc[...] = new

    @pl.when((phase == 1) & (step == 0))
    def _():
        acc_sc[...] = jnp.zeros(acc_sc.shape, jnp.float32)

    @pl.when(phase == 1)
    def _():
        probs = jnp.exp(scores - m_sc[...]) * (1.0 / l_sc[...])
        acc_sc[...] += jnp.dot(probs.astype(jnp.bfloat16), v_ref[...], preferred_element_type=jnp.float32)

    @pl.when((phase == 1) & (step == steps - 1))
    def _():
        att_ref[...] = acc_sc[...]
        m_ref[...] = jnp.broadcast_to(m_sc[...], m_ref.shape)
        l_ref[...] = jnp.broadcast_to(l_sc[...], l_ref.shape)


def backward_kernel(
    flag_ref, q_ref, k_ref, v_ref, g_ref, att_ref, m_ref, l_ref, dq_ref, dk_ref, dv_ref, dq_sc, *, tiles, steps, scale
):
    step = pl.program_id(1)
    q = q_ref[...]
    k = k_ref[...]
    g = g_ref[...]
    scores = masked_scores(flag_ref, q, k, step, tiles, scale)
    probs = jnp.exp(scores - m_ref[:, :1]) * (1.0 / l_ref[:, :1])
    weights = probs.astype(jnp.bfloat16)
    dots = lax.dot_general(g, v_ref[...], (((1,), (1,)), ((), ())), preferred_element_type=jnp.float32)
    delta = jnp.sum(g.astype(jnp.float32) * att_ref[...], axis=1, keepdims=True)
    slopes = (probs * (dots - delta) * scale).astype(jnp.bfloat16)

    @pl.when(step == 0)
    def _():
        dq_sc[...] = jnp.zeros(dq_sc.shape, jnp.float32)

    dq_sc[...] += jnp.dot(slopes, k, preferred_element_type=jnp.float32)
    dk_ref[...] = lax.dot_general(slopes, q, (((0,), (0,)), ((), ())), preferred_element_type=jnp.float32)
    dv_ref[...] = lax.dot_general(weights, g, (((0,), (0,)), ((), ())), preferred_element_type=jnp.float32)

    @pl.when(step == steps - 1)
    def _():
        dq_ref[...] = dq_sc[...]


def attention_forward(flags, queries, keys_all, values_all, scale):
    nblocks, block_len, cols = keys_all.shape
    heads = cols // DH
    tiles = block_len // KEY_TILE
    steps = nblocks * tiles
    q_spec = pl.BlockSpec((block_len, DH), lambda h, ph, s, f: (0, h))
    k_spec = pl.BlockSpec((None, KEY_TILE, DH), lambda h, ph, s, f: (s // tiles, s % tiles, h))
    v_spec = pl.BlockSpec((None, KEY_TILE, DH), lambda h, ph, s, f: ((s // tiles) * ph, (s % tiles) * ph, h))
    stat_spec = pl.BlockSpec((None, block_len, DH), lambda h, ph, s, f: (h, 0, 0))
    kernel = functools.partial(forward_kernel, tiles=tiles, steps=steps, scale=scale)
    return pl.pallas_call(
        kernel,
        grid_spec=pltpu.PrefetchScalarGridSpec(
            num_scalar_prefetch=1,
            grid=(heads, 2, steps),
            in_specs=[q_spec, k_spec, v_spec],
            out_specs=[q_spec, stat_spec, stat_spec],
            scratch_shapes=[
                pltpu.VMEM((block_len, 1), jnp.float32),
                pltpu.VMEM((block_len, 1), jnp.float32),
                pltpu.VMEM((block_len, DH), jnp.float32),
            ],
        ),
        out_shape=[
            jax.ShapeDtypeStruct((block_len, cols), jnp.float32),
            jax.ShapeDtypeStruct((heads, block_len, DH), jnp.float32),
            jax.ShapeDtypeStruct((heads, block_len, DH), jnp.float32),
        ],
        compiler_params=pltpu.CompilerParams(dimension_semantics=("arbitrary", "arbitrary", "arbitrary")),
    )(flags, queries, keys_all, values_all)


def attention_backward(flags, queries, keys_all, values_all, grads, attended32, row_max, row_total, scale):
    nblocks, block_len, cols = keys_all.shape
    heads = cols // DH
    tiles = block_len // KEY_TILE
    steps = nblocks * tiles
    q_spec = pl.BlockSpec((block_len, DH), lambda h, s, f: (0, h))
    k_spec = pl.BlockSpec((None, KEY_TILE, DH), lambda h, s, f: (s // tiles, s % tiles, h))
    stat_spec = pl.BlockSpec((None, block_len, DH), lambda h, s, f: (h, 0, 0))
    kernel = functools.partial(backward_kernel, tiles=tiles, steps=steps, scale=scale)
    return pl.pallas_call(
        kernel,
        grid_spec=pltpu.PrefetchScalarGridSpec(
            num_scalar_prefetch=1,
            grid=(heads, steps),
            in_specs=[q_spec, k_spec, k_spec, q_spec, q_spec, stat_spec, stat_spec],
            out_specs=[q_spec, k_spec, k_spec],
            scratch_shapes=[pltpu.VMEM((block_len, DH), jnp.float32)],
        ),
        out_shape=[
            jax.ShapeDtypeStruct((block_len, cols), jnp.float32),
            jax.ShapeDtypeStruct((nblocks, block_len, cols), jnp.float32),
            jax.ShapeDtypeStruct((nblocks, block_len, cols), jnp.float32),
        ],
        compiler_params=pltpu.CompilerParams(dimension_semantics=("arbitrary", "arbitrary")),
    )(flags, queries, keys_all, values_all, grads, attended32, row_max, row_total)


def local(queries, keys, values, out_weight, cotangent, block_keep):
    block_len = queries.shape[0]
    local_cols = queries.shape[1]
    score_scale = 1.0 / math.sqrt(DH)
    axis_len = lax.axis_size("ctx")
    levels = axis_len.bit_length() - 1
    block_index = lax.axis_index("ctx")
    stacked = jnp.stack([keys, values])
    remote = [passed_along(stacked, "ctx", 1 << level) for level in range(levels)]
    blocks = [stacked] + remote
    keys_all = jnp.stack([b[0] for b in blocks])
    values_all = jnp.stack([b[1] for b in blocks])
    row_pick = lax.broadcasted_iota(jnp.int32, block_keep.shape, 0) == block_index
    keep_row = jnp.sum(jnp.where(row_pick, block_keep, 0), axis=0)
    column_ids = lax.broadcasted_iota(jnp.int32, keep_row.shape, 0)
    flags = [jnp.array(True)]
    for level in range(levels):
        target = block_index - (1 << level)
        linked = jnp.sum(jnp.where(column_ids == target, keep_row, 0))
        flags.append((target >= 0) & (linked == 1))
    flags = jnp.stack(flags).astype(jnp.int32)

    attended32, row_max, row_total = attention_forward(flags, queries, keys_all, values_all, score_scale)
    attended = attended32.astype(jnp.bfloat16)
    weight_cols = lax.all_to_all(out_weight, "tp", split_axis=1, concat_axis=0, tiled=True)
    mixed_sum = jnp.dot(gathered(attended, "tp"), weight_cols, preferred_element_type=jnp.float32)
    mixed = mixed_sum.astype(jnp.bfloat16)
    piece = gathered(cotangent, "tp")
    grad_att = lax.dot_general(
        piece, out_weight, (((1,), (1,)), ((), ())), preferred_element_type=jnp.float32
    )
    weight_part = lax.dot_general(
        attended, piece, (((0,), (0,)), ((), ())), preferred_element_type=jnp.float32
    )
    d_weight = summed_scatter(weight_part.astype(jnp.bfloat16), "ctx")
    grad_heads = grad_att.astype(jnp.bfloat16)
    grad_query, key_grads, value_grads = attention_backward(
        flags, queries, keys_all, values_all, grad_heads, attended32, row_max, row_total, score_scale
    )
    own_key = key_grads[0]
    own_value = value_grads[0]
    for level in range(levels):
        back = jnp.stack([key_grads[level + 1], value_grads[level + 1]]).astype(jnp.bfloat16)
        arrived = passed_along(back, "ctx", -(1 << level)).astype(jnp.float32)
        own_key = own_key + arrived[0]
        own_value = own_value + arrived[1]
    return (mixed, grad_query, own_key, own_value, d_weight)


def solution(mesh):
    in_specs = (P("ctx", "tp"), P("ctx", "tp"), P("ctx", "tp"), P("tp", None), P("ctx", "tp"), P())
    out_specs = (P("ctx", "tp"), P("ctx", "tp"), P("ctx", "tp"), P("ctx", "tp"), P("tp", "ctx"))
    return jax.shard_map(local, mesh=mesh, in_specs=in_specs, out_specs=out_specs, check_vma=False)
```

```python
import functools
import math

import jax
import jax.numpy as jnp
from jax import lax
from jax.experimental import pallas as pl
from jax.experimental.pallas import tpu as pltpu
from jax.sharding import PartitionSpec as P

DH = 128
NEG = -1e30
KEY_TILE = 512


def passed_along(value, axis, steps):
    count = lax.axis_size(axis)
    initial, last = (max(0, -steps), min(count, count - steps))
    return lax.ppermute(value, axis, [(source, source + steps) for source in range(initial, last)])


def gathered(piece, axis):
    count = lax.axis_size(axis)
    spread = jnp.broadcast_to(piece[None], (count,) + piece.shape)
    parts = lax.all_to_all(spread, axis, 0, 0, tiled=True)
    return jnp.moveaxis(parts, 0, 1).reshape(piece.shape[0], count * piece.shape[1])


def summed_scatter(part, axis):
    count = lax.axis_size(axis)
    rows, cols = part.shape
    pieces = part.reshape(rows, count, cols // count)
    parts = lax.all_to_all(pieces, axis, 1, 1, tiled=True)
    return jnp.sum(parts.astype(jnp.float32), axis=1)


def masked_scores(flag_ref, q, k, step, tiles, scale):
    block = step // tiles
    tile = step % tiles
    raw = lax.dot_general(q, k, (((1,), (1,)), ((), ())), preferred_element_type=jnp.float32) * scale
    rows = lax.broadcasted_iota(jnp.int32, raw.shape, 0)
    cols = lax.broadcasted_iota(jnp.int32, raw.shape, 1) + tile * raw.shape[1]
    reach = 1 << 20
    offset = jnp.where(block == 0, 0, jnp.where(flag_ref[block] == 1, reach, -reach))
    return jnp.where(rows + offset >= cols, raw, NEG)


def forward_kernel(flag_ref, q_ref, k_ref, v_ref, att_ref, m_ref, l_ref, m_sc, l_sc, acc_sc, *, tiles, steps, scale):
    phase = pl.program_id(1)
    step = pl.program_id(2)
    scores = masked_scores(flag_ref, q_ref[...], k_ref[...], step, tiles, scale)

    @pl.when((phase == 0) & (step == 0))
    def _():
        m_sc[...] = jnp.full(m_sc.shape, NEG, jnp.float32)
        l_sc[...] = jnp.zeros(l_sc.shape, jnp.float32)

    @pl.when(phase == 0)
    def _():
        old = m_sc[...]
        new = jnp.maximum(old, jnp.max(scores, axis=1, keepdims=True))
        l_sc[...] = l_sc[...] * jnp.exp(old - new) + jnp.sum(jnp.exp(scores - new), axis=1, keepdims=True)
        m_sc[...] = new

    @pl.when((phase == 1) & (step == 0))
    def _():
        acc_sc[...] = jnp.zeros(acc_sc.shape, jnp.float32)

    @pl.when(phase == 1)
    def _():
        probs = jnp.exp(scores - m_sc[...]) * (1.0 / l_sc[...])
        acc_sc[...] += jnp.dot(probs.astype(jnp.bfloat16), v_ref[...], preferred_element_type=jnp.float32)

    @pl.when((phase == 1) & (step == steps - 1))
    def _():
        att_ref[...] = acc_sc[...]
        m_ref[...] = jnp.broadcast_to(m_sc[...], m_ref.shape)
        l_ref[...] = jnp.broadcast_to(l_sc[...], l_ref.shape)


def backward_kernel(
    flag_ref, q_ref, k_ref, v_ref, g_ref, att_ref, m_ref, l_ref, dq_ref, dk_ref, dv_ref, dq_sc, *, tiles, steps, scale
):
    step = pl.program_id(1)
    q = q_ref[...]
    k = k_ref[...]
    g = g_ref[...]
    scores = masked_scores(flag_ref, q, k, step, tiles, scale)
    probs = jnp.exp(scores - m_ref[:, :1]) * (1.0 / l_ref[:, :1])
    weights = probs.astype(jnp.bfloat16)
    dots = lax.dot_general(g, v_ref[...], (((1,), (1,)), ((), ())), preferred_element_type=jnp.float32)
    delta = jnp.sum(g.astype(jnp.float32) * att_ref[...], axis=1, keepdims=True)
    slopes = (probs * (dots - delta) * scale).astype(jnp.bfloat16)

    @pl.when(step == 0)
    def _():
        dq_sc[...] = jnp.zeros(dq_sc.shape, jnp.float32)

    dq_sc[...] += jnp.dot(slopes, k, preferred_element_type=jnp.float32)
    dk_ref[...] = lax.dot_general(slopes, q, (((0,), (0,)), ((), ())), preferred_element_type=jnp.float32)
    dv_ref[...] = lax.dot_general(weights, g, (((0,), (0,)), ((), ())), preferred_element_type=jnp.float32)

    @pl.when(step == steps - 1)
    def _():
        dq_ref[...] = dq_sc[...]


def attention_forward(flags, queries, keys_all, values_all, scale):
    nblocks, block_len, cols = keys_all.shape
    heads = cols // DH
    tiles = block_len // KEY_TILE
    steps = nblocks * tiles
    q_spec = pl.BlockSpec((block_len, DH), lambda h, ph, s, f: (0, h))
    k_spec = pl.BlockSpec((None, KEY_TILE, DH), lambda h, ph, s, f: (s // tiles, s % tiles, h))
    v_spec = pl.BlockSpec((None, KEY_TILE, DH), lambda h, ph, s, f: ((s // tiles) * ph, (s % tiles) * ph, h))
    stat_spec = pl.BlockSpec((None, block_len, DH), lambda h, ph, s, f: (h, 0, 0))
    kernel = functools.partial(forward_kernel, tiles=tiles, steps=steps, scale=scale)
    return pl.pallas_call(
        kernel,
        grid_spec=pltpu.PrefetchScalarGridSpec(
            num_scalar_prefetch=1,
            grid=(heads, 2, steps),
            in_specs=[q_spec, k_spec, v_spec],
            out_specs=[q_spec, stat_spec, stat_spec],
            scratch_shapes=[
                pltpu.VMEM((block_len, 1), jnp.float32),
                pltpu.VMEM((block_len, 1), jnp.float32),
                pltpu.VMEM((block_len, DH), jnp.float32),
            ],
        ),
        out_shape=[
            jax.ShapeDtypeStruct((block_len, cols), jnp.float32),
            jax.ShapeDtypeStruct((heads, block_len, DH), jnp.float32),
            jax.ShapeDtypeStruct((heads, block_len, DH), jnp.float32),
        ],
        compiler_params=pltpu.CompilerParams(dimension_semantics=("arbitrary", "arbitrary", "arbitrary")),
    )(flags, queries, keys_all, values_all)


def attention_backward(flags, queries, keys_all, values_all, grads, attended32, row_max, row_total, scale):
    nblocks, block_len, cols = keys_all.shape
    heads = cols // DH
    tiles = block_len // KEY_TILE
    steps = nblocks * tiles
    q_spec = pl.BlockSpec((block_len, DH), lambda h, s, f: (0, h))
    k_spec = pl.BlockSpec((None, KEY_TILE, DH), lambda h, s, f: (s // tiles, s % tiles, h))
    stat_spec = pl.BlockSpec((None, block_len, DH), lambda h, s, f: (h, 0, 0))
    kernel = functools.partial(backward_kernel, tiles=tiles, steps=steps, scale=scale)
    return pl.pallas_call(
        kernel,
        grid_spec=pltpu.PrefetchScalarGridSpec(
            num_scalar_prefetch=1,
            grid=(heads, steps),
            in_specs=[q_spec, k_spec, k_spec, q_spec, q_spec, stat_spec, stat_spec],
            out_specs=[q_spec, k_spec, k_spec],
            scratch_shapes=[pltpu.VMEM((block_len, DH), jnp.float32)],
        ),
        out_shape=[
            jax.ShapeDtypeStruct((block_len, cols), jnp.float32),
            jax.ShapeDtypeStruct((nblocks, block_len, cols), jnp.float32),
            jax.ShapeDtypeStruct((nblocks, block_len, cols), jnp.float32),
        ],
        compiler_params=pltpu.CompilerParams(dimension_semantics=("arbitrary", "arbitrary")),
    )(flags, queries, keys_all, values_all, grads, attended32, row_max, row_total)


def local(queries, keys, values, out_weight, cotangent, block_keep):
    block_len = queries.shape[0]
    local_cols = queries.shape[1]
    score_scale = 1.0 / math.sqrt(DH)
    axis_len = lax.axis_size("ctx")
    levels = axis_len.bit_length() - 1
    block_index = lax.axis_index("ctx")
    stacked = jnp.stack([keys, values])
    remote = [passed_along(stacked, "ctx", 1 << level) for level in range(levels)]
    blocks = [stacked] + remote
    keys_all = jnp.stack([b[0] for b in blocks])
    values_all = jnp.stack([b[1] for b in blocks])
    row_pick = lax.broadcasted_iota(jnp.int32, block_keep.shape, 0) == block_index
    keep_row = jnp.sum(jnp.where(row_pick, block_keep, 0), axis=0)
    column_ids = lax.broadcasted_iota(jnp.int32, keep_row.shape, 0)
    flags = [jnp.array(True)]
    for level in range(levels):
        target = block_index - (1 << level)
        linked = jnp.sum(jnp.where(column_ids == target, keep_row, 0))
        flags.append((target >= 0) & (linked == 1))
    flags = jnp.stack(flags).astype(jnp.int32)

    tp_len = lax.axis_size("tp")
    tp_index = lax.axis_index("tp")
    weight_cols = lax.all_to_all(out_weight, "tp", split_axis=1, concat_axis=0, tiled=True)
    grad_part = lax.dot_general(
        cotangent, weight_cols, (((1,), (1,)), ((), ())), preferred_element_type=jnp.float32
    )
    grad_parts = lax.all_to_all(
        grad_part.astype(jnp.bfloat16).reshape(block_len, tp_len, local_cols), "tp", 1, 1, tiled=True
    )
    grad_heads = jnp.sum(grad_parts.astype(jnp.float32), axis=1).astype(jnp.bfloat16)

    attended32, row_max, row_total = attention_forward(flags, queries, keys_all, values_all, score_scale)
    attended = attended32.astype(jnp.bfloat16)
    spread = jnp.broadcast_to(attended[None], (tp_len,) + attended.shape)
    att_parts = lax.all_to_all(spread, "tp", 0, 0, tiled=True)
    mixed_sum = jnp.einsum(
        "ktc,kcf->tf",
        att_parts,
        weight_cols.reshape(tp_len, local_cols, weight_cols.shape[1]),
        preferred_element_type=jnp.float32,
    )
    mixed = mixed_sum.astype(jnp.bfloat16)
    weight_part = jnp.einsum("ktc,tf->kcf", att_parts, cotangent, preferred_element_type=jnp.float32)
    halves = cotangent.shape[1] // local_cols
    pieces = (
        weight_part.astype(jnp.bfloat16)
        .reshape(tp_len, local_cols, halves, local_cols)
        .transpose(0, 2, 1, 3)
        .reshape(tp_len * halves, local_cols, local_cols)
    )
    reduced = jnp.sum(lax.all_to_all(pieces, "ctx", 0, 0, tiled=True).astype(jnp.float32), axis=0)
    moves = []
    for k in range(axis_len):
        for p in range(tp_len):
            moves.append((k * tp_len + p, (halves * p + k % halves) * tp_len + k // halves))
    d_weight = lax.ppermute(reduced, ("ctx", "tp"), moves)
    grad_query, key_grads, value_grads = attention_backward(
        flags, queries, keys_all, values_all, grad_heads, attended32, row_max, row_total, score_scale
    )
    own_key = key_grads[0]
    own_value = value_grads[0]
    for level in range(levels):
        back = jnp.stack([key_grads[level + 1], value_grads[level + 1]]).astype(jnp.bfloat16)
        arrived = passed_along(back, "ctx", -(1 << level)).astype(jnp.float32)
        own_key = own_key + arrived[0]
        own_value = own_value + arrived[1]
    return (mixed, grad_query, own_key, own_value, d_weight)


def solution(mesh):
    in_specs = (P("ctx", "tp"), P("ctx", "tp"), P("ctx", "tp"), P("tp", None), P("ctx", "tp"), P())
    out_specs = (P("ctx", "tp"), P("ctx", "tp"), P("ctx", "tp"), P("ctx", "tp"), P("tp", "ctx"))
    return jax.shard_map(local, mesh=mesh, in_specs=in_specs, out_specs=out_specs, check_vma=False)
```

```python
import functools
import math

import jax
import jax.numpy as jnp
from jax import lax
from jax.experimental import pallas as pl
from jax.experimental.pallas import tpu as pltpu
from jax.sharding import PartitionSpec as P

DH = 128
NEG = -1e30
KEY_TILE = 512


def passed_along(value, axis, steps):
    count = lax.axis_size(axis)
    initial, last = (max(0, -steps), min(count, count - steps))
    return lax.ppermute(value, axis, [(source, source + steps) for source in range(initial, last)])


def masked_scores(flag_ref, q, k, step, tiles, scale):
    block = step // tiles
    tile = step % tiles
    raw = lax.dot_general(q, k, (((1,), (1,)), ((), ())), preferred_element_type=jnp.float32) * scale
    rows = lax.broadcasted_iota(jnp.int32, raw.shape, 0)
    cols = lax.broadcasted_iota(jnp.int32, raw.shape, 1) + tile * raw.shape[1]
    reach = 1 << 20
    offset = jnp.where(block == 0, 0, jnp.where(flag_ref[block] == 1, reach, -reach))
    return jnp.where(rows + offset >= cols, raw, NEG)


def forward_kernel(flag_ref, q_ref, k_ref, v_ref, after_ref, att_ref, m_ref, l_ref, m_sc, l_sc, acc_sc, *, tiles, steps, scale):
    phase = pl.program_id(1)
    step = pl.program_id(2)
    scores = masked_scores(flag_ref, q_ref[...], k_ref[...], step, tiles, scale)

    @pl.when((phase == 0) & (step == 0))
    def _():
        m_sc[...] = jnp.full(m_sc.shape, NEG, jnp.float32)
        l_sc[...] = jnp.zeros(l_sc.shape, jnp.float32)

    @pl.when(phase == 0)
    def _():
        old = m_sc[...]
        new = jnp.maximum(old, jnp.max(scores, axis=1, keepdims=True))
        l_sc[...] = l_sc[...] * jnp.exp(old - new) + jnp.sum(jnp.exp(scores - new), axis=1, keepdims=True)
        m_sc[...] = new

    @pl.when((phase == 1) & (step == 0))
    def _():
        acc_sc[...] = jnp.zeros(acc_sc.shape, jnp.float32)

    @pl.when(phase == 1)
    def _():
        probs = jnp.exp(scores - m_sc[...]) * (1.0 / l_sc[...])
        acc_sc[...] += jnp.dot(probs.astype(jnp.bfloat16), v_ref[...], preferred_element_type=jnp.float32)

    @pl.when((phase == 1) & (step == steps - 1))
    def _():
        att_ref[...] = acc_sc[...]
        m_ref[...] = jnp.broadcast_to(m_sc[...], m_ref.shape)
        l_ref[...] = jnp.broadcast_to(l_sc[...], l_ref.shape)


def backward_kernel(
    flag_ref, q_ref, k_ref, v_ref, g_ref, att_ref, m_ref, l_ref, dq_ref, dk_ref, dv_ref, dq_sc, *, tiles, steps, scale
):
    step = pl.program_id(1)
    q = q_ref[...]
    k = k_ref[...]
    g = g_ref[...]
    scores = masked_scores(flag_ref, q, k, step, tiles, scale)
    probs = jnp.exp(scores - m_ref[:, :1]) * (1.0 / l_ref[:, :1])
    weights = probs.astype(jnp.bfloat16)
    dots = lax.dot_general(g, v_ref[...], (((1,), (1,)), ((), ())), preferred_element_type=jnp.float32)
    delta = jnp.sum(g.astype(jnp.float32) * att_ref[...], axis=1, keepdims=True)
    slopes = (probs * (dots - delta) * scale).astype(jnp.bfloat16)

    @pl.when(step == 0)
    def _():
        dq_sc[...] = jnp.zeros(dq_sc.shape, jnp.float32)

    dq_sc[...] += jnp.dot(slopes, k, preferred_element_type=jnp.float32)
    dk_ref[...] = lax.dot_general(slopes, q, (((0,), (0,)), ((), ())), preferred_element_type=jnp.float32)
    dv_ref[...] = lax.dot_general(weights, g, (((0,), (0,)), ((), ())), preferred_element_type=jnp.float32)

    @pl.when(step == steps - 1)
    def _():
        dq_ref[...] = dq_sc[...]


def attention_forward(flags, queries, keys_all, values_all, after, scale):
    nblocks, block_len, cols = keys_all.shape
    heads = cols // DH
    tiles = block_len // KEY_TILE
    steps = nblocks * tiles
    q_spec = pl.BlockSpec((block_len, DH), lambda h, ph, s, f: (0, h))
    k_spec = pl.BlockSpec((None, KEY_TILE, DH), lambda h, ph, s, f: (s // tiles, s % tiles, h))
    v_spec = pl.BlockSpec((None, KEY_TILE, DH), lambda h, ph, s, f: ((s // tiles) * ph, (s % tiles) * ph, h))
    stat_spec = pl.BlockSpec((None, block_len, DH), lambda h, ph, s, f: (h, 0, 0))
    kernel = functools.partial(forward_kernel, tiles=tiles, steps=steps, scale=scale)
    return pl.pallas_call(
        kernel,
        grid_spec=pltpu.PrefetchScalarGridSpec(
            num_scalar_prefetch=1,
            grid=(heads, 2, steps),
            in_specs=[q_spec, k_spec, v_spec, pl.BlockSpec(memory_space=pl.ANY)],
            out_specs=[q_spec, stat_spec, stat_spec],
            scratch_shapes=[
                pltpu.VMEM((block_len, 1), jnp.float32),
                pltpu.VMEM((block_len, 1), jnp.float32),
                pltpu.VMEM((block_len, DH), jnp.float32),
            ],
        ),
        out_shape=[
            jax.ShapeDtypeStruct((block_len, cols), jnp.float32),
            jax.ShapeDtypeStruct((heads, block_len, DH), jnp.float32),
            jax.ShapeDtypeStruct((heads, block_len, DH), jnp.float32),
        ],
        compiler_params=pltpu.CompilerParams(dimension_semantics=("arbitrary", "arbitrary", "arbitrary")),
    )(flags, queries, keys_all, values_all, after)


def attention_backward(flags, queries, keys_all, values_all, grads, attended32, row_max, row_total, scale):
    nblocks, block_len, cols = keys_all.shape
    heads = cols // DH
    tiles = block_len // KEY_TILE
    steps = nblocks * tiles
    q_spec = pl.BlockSpec((block_len, DH), lambda h, s, f: (0, h))
    k_spec = pl.BlockSpec((None, KEY_TILE, DH), lambda h, s, f: (s // tiles, s % tiles, h))
    stat_spec = pl.BlockSpec((None, block_len, DH), lambda h, s, f: (h, 0, 0))
    kernel = functools.partial(backward_kernel, tiles=tiles, steps=steps, scale=scale)
    return pl.pallas_call(
        kernel,
        grid_spec=pltpu.PrefetchScalarGridSpec(
            num_scalar_prefetch=1,
            grid=(heads, steps),
            in_specs=[q_spec, k_spec, k_spec, q_spec, q_spec, stat_spec, stat_spec],
            out_specs=[q_spec, k_spec, k_spec],
            scratch_shapes=[pltpu.VMEM((block_len, DH), jnp.float32)],
        ),
        out_shape=[
            jax.ShapeDtypeStruct((block_len, cols), jnp.float32),
            jax.ShapeDtypeStruct((nblocks, block_len, cols), jnp.float32),
            jax.ShapeDtypeStruct((nblocks, block_len, cols), jnp.float32),
        ],
        compiler_params=pltpu.CompilerParams(dimension_semantics=("arbitrary", "arbitrary")),
    )(flags, queries, keys_all, values_all, grads, attended32, row_max, row_total)


def local(queries, keys, values, out_weight, cotangent, block_keep):
    block_len = queries.shape[0]
    local_cols = queries.shape[1]
    score_scale = 1.0 / math.sqrt(DH)
    axis_len = lax.axis_size("ctx")
    levels = axis_len.bit_length() - 1
    block_index = lax.axis_index("ctx")
    stacked = jnp.stack([keys, values])
    remote = [passed_along(stacked, "ctx", 1 << level) for level in range(levels)]
    blocks = [stacked] + remote
    keys_all = jnp.stack([b[0] for b in blocks])
    values_all = jnp.stack([b[1] for b in blocks])
    row_pick = lax.broadcasted_iota(jnp.int32, block_keep.shape, 0) == block_index
    keep_row = jnp.sum(jnp.where(row_pick, block_keep, 0), axis=0)
    column_ids = lax.broadcasted_iota(jnp.int32, keep_row.shape, 0)
    flags = [jnp.array(True)]
    for level in range(levels):
        target = block_index - (1 << level)
        linked = jnp.sum(jnp.where(column_ids == target, keep_row, 0))
        flags.append((target >= 0) & (linked == 1))
    flags = jnp.stack(flags).astype(jnp.int32)

    tp_len = lax.axis_size("tp")
    tp_index = lax.axis_index("tp")
    weight_cols = lax.all_to_all(out_weight, "tp", split_axis=1, concat_axis=0, tiled=True)
    grad_part = lax.dot_general(
        cotangent, weight_cols, (((1,), (1,)), ((), ())), preferred_element_type=jnp.float32
    )
    grad_parts = lax.all_to_all(
        grad_part.astype(jnp.bfloat16).reshape(block_len, tp_len, local_cols), "tp", 1, 1, tiled=True
    )
    grad_heads = jnp.sum(grad_parts.astype(jnp.float32), axis=1).astype(jnp.bfloat16)

    attended32, row_max, row_total = attention_forward(
        flags, queries, keys_all, values_all, grad_heads, score_scale
    )
    attended = attended32.astype(jnp.bfloat16)
    spread = jnp.broadcast_to(attended[None], (tp_len,) + attended.shape)
    att_parts = lax.all_to_all(spread, "tp", 0, 0, tiled=True)
    mixed_sum = jnp.einsum(
        "ktc,kcf->tf",
        att_parts,
        weight_cols.reshape(tp_len, local_cols, weight_cols.shape[1]),
        preferred_element_type=jnp.float32,
    )
    mixed = mixed_sum.astype(jnp.bfloat16)
    weight_part = jnp.einsum("ktc,tf->kcf", att_parts, cotangent, preferred_element_type=jnp.float32)
    halves = cotangent.shape[1] // local_cols
    pieces = (
        weight_part.astype(jnp.bfloat16)
        .reshape(tp_len, local_cols, halves, local_cols)
        .transpose(0, 2, 1, 3)
        .reshape(tp_len * halves, local_cols, local_cols)
    )
    reduced = jnp.sum(lax.all_to_all(pieces, "ctx", 0, 0, tiled=True).astype(jnp.float32), axis=0)
    moves = []
    for k in range(axis_len):
        for p in range(tp_len):
            moves.append((k * tp_len + p, (halves * p + k % halves) * tp_len + k // halves))
    d_weight = lax.ppermute(reduced, ("ctx", "tp"), moves)
    grad_query, key_grads, value_grads = attention_backward(
        flags, queries, keys_all, values_all, grad_heads, attended32, row_max, row_total, score_scale
    )
    own_key = key_grads[0]
    own_value = value_grads[0]
    for level in range(levels):
        back = jnp.stack([key_grads[level + 1], value_grads[level + 1]]).astype(jnp.bfloat16)
        arrived = passed_along(back, "ctx", -(1 << level)).astype(jnp.float32)
        own_key = own_key + arrived[0]
        own_value = own_value + arrived[1]
    return (mixed, grad_query, own_key, own_value, d_weight)


def solution(mesh):
    in_specs = (P("ctx", "tp"), P("ctx", "tp"), P("ctx", "tp"), P("tp", None), P("ctx", "tp"), P())
    out_specs = (P("ctx", "tp"), P("ctx", "tp"), P("ctx", "tp"), P("ctx", "tp"), P("tp", "ctx"))
    return jax.shard_map(local, mesh=mesh, in_specs=in_specs, out_specs=out_specs, check_vma=False)
```

```python
import functools
import math

import jax
import jax.numpy as jnp
from jax import lax
from jax.experimental import pallas as pl
from jax.experimental.pallas import tpu as pltpu
from jax.sharding import PartitionSpec as P

DH = 128
NEG = -1e30
KEY_TILE = 512
FORWARD_ORDER = (0, 2, 1, 3)
BACKWARD_ORDER = (3, 1, 2, 0)


def passed_along(value, axis, steps):
    count = lax.axis_size(axis)
    initial, last = (max(0, -steps), min(count, count - steps))
    return lax.ppermute(value, axis, [(source, source + steps) for source in range(initial, last)])


def block_scores(q, k, tile, causal, scale):
    raw = lax.dot_general(q, k, (((1,), (1,)), ((), ())), preferred_element_type=jnp.float32) * scale
    if not causal:
        return raw
    rows = lax.broadcasted_iota(jnp.int32, raw.shape, 0)
    cols = lax.broadcasted_iota(jnp.int32, raw.shape, 1) + tile * raw.shape[1]
    return jnp.where(rows >= cols, raw, NEG)


def forward_kernel(flag_ref, *refs, causal, first, tiles, scale, waits):
    refs = refs[:3] + refs[3 + waits:]
    if first:
        q_ref, k_ref, v_ref, m_ref, l_ref, acc_ref, m_sc, l_sc, acc_sc = refs
    else:
        q_ref, k_ref, v_ref, m_in, l_in, acc_in, m_ref, l_ref, acc_ref, m_sc, l_sc, acc_sc = refs
    tile = pl.program_id(1)

    @pl.when(tile == 0)
    def _():
        if first:
            m_sc[...] = jnp.full(m_sc.shape, NEG, jnp.float32)
            l_sc[...] = jnp.zeros(l_sc.shape, jnp.float32)
            acc_sc[...] = jnp.zeros(acc_sc.shape, jnp.float32)
        else:
            m_sc[...] = m_in[:, :1]
            l_sc[...] = l_in[:, :1]
            acc_sc[...] = acc_in[...]

    @pl.when(flag_ref[0] == 1)
    def _():
        scores = block_scores(q_ref[...], k_ref[...], tile, causal, scale)
        old = m_sc[...]
        new = jnp.maximum(old, jnp.max(scores, axis=1, keepdims=True))
        alpha = jnp.exp(old - new)
        expd = jnp.exp(scores - new)
        l_sc[...] = l_sc[...] * alpha + jnp.sum(expd, axis=1, keepdims=True)
        acc_sc[...] = acc_sc[...] * alpha + jnp.dot(
            expd.astype(jnp.bfloat16), v_ref[...], preferred_element_type=jnp.float32
        )
        m_sc[...] = new

    @pl.when(tile == tiles - 1)
    def _():
        m_ref[...] = jnp.broadcast_to(m_sc[...], m_ref.shape)
        l_ref[...] = jnp.broadcast_to(l_sc[...], l_ref.shape)
        acc_ref[...] = acc_sc[...]


def forward_block(flag, queries, keys, values, state, causal, scale, after=()):
    block_len, cols = queries.shape
    heads = cols // DH
    tiles = block_len // KEY_TILE
    first = state is None
    row_spec = pl.BlockSpec((block_len, DH), lambda h, t, f: (0, h))
    key_spec = pl.BlockSpec((KEY_TILE, DH), lambda h, t, f: (t, h))
    in_specs = [row_spec, key_spec, key_spec] + [pl.BlockSpec(memory_space=pl.ANY)] * len(after)
    operands = [queries, keys, values] + list(after)
    if not first:
        in_specs += [row_spec, row_spec, row_spec]
        operands += list(state)
    kernel = functools.partial(
        forward_kernel, causal=causal, first=first, tiles=tiles, scale=scale, waits=len(after)
    )
    return pl.pallas_call(
        kernel,
        grid_spec=pltpu.PrefetchScalarGridSpec(
            num_scalar_prefetch=1,
            grid=(heads, tiles),
            in_specs=in_specs,
            out_specs=[row_spec, row_spec, row_spec],
            scratch_shapes=[
                pltpu.VMEM((block_len, 1), jnp.float32),
                pltpu.VMEM((block_len, 1), jnp.float32),
                pltpu.VMEM((block_len, DH), jnp.float32),
            ],
        ),
        out_shape=[jax.ShapeDtypeStruct((block_len, cols), jnp.float32)] * 3,
        compiler_params=pltpu.CompilerParams(dimension_semantics=("arbitrary", "arbitrary")),
    )(flag, *operands)


def backward_kernel(flag_ref, *refs, causal, tiles, scale, waits):
    refs = refs[:7] + refs[7 + waits:]
    q_ref, k_ref, v_ref, g_ref, att_ref, m_ref, l_ref, dq_ref, dk_ref, dv_ref, dq_sc = refs
    tile = pl.program_id(1)

    @pl.when(tile == 0)
    def _():
        dq_sc[...] = jnp.zeros(dq_sc.shape, jnp.float32)

    @pl.when(flag_ref[0] == 1)
    def _():
        q = q_ref[...]
        k = k_ref[...]
        g = g_ref[...]
        scores = block_scores(q, k, tile, causal, scale)
        probs = jnp.exp(scores - m_ref[:, :1]) * (1.0 / l_ref[:, :1])
        weights = probs.astype(jnp.bfloat16)
        dots = lax.dot_general(g, v_ref[...], (((1,), (1,)), ((), ())), preferred_element_type=jnp.float32)
        delta = jnp.sum(g.astype(jnp.float32) * att_ref[...], axis=1, keepdims=True)
        slopes = (probs * (dots - delta) * scale).astype(jnp.bfloat16)
        dq_sc[...] += jnp.dot(slopes, k, preferred_element_type=jnp.float32)
        dk_ref[...] = lax.dot_general(slopes, q, (((0,), (0,)), ((), ())), preferred_element_type=jnp.float32)
        dv_ref[...] = lax.dot_general(weights, g, (((0,), (0,)), ((), ())), preferred_element_type=jnp.float32)

    @pl.when(flag_ref[0] != 1)
    def _():
        dk_ref[...] = jnp.zeros(dk_ref.shape, jnp.float32)
        dv_ref[...] = jnp.zeros(dv_ref.shape, jnp.float32)

    @pl.when(tile == tiles - 1)
    def _():
        dq_ref[...] = dq_sc[...]


def backward_block(flag, queries, keys, values, grads, attended32, row_max, row_total, causal, scale, after=()):
    block_len, cols = queries.shape
    heads = cols // DH
    tiles = block_len // KEY_TILE
    row_spec = pl.BlockSpec((block_len, DH), lambda h, t, f: (0, h))
    key_spec = pl.BlockSpec((KEY_TILE, DH), lambda h, t, f: (t, h))
    kernel = functools.partial(backward_kernel, causal=causal, tiles=tiles, scale=scale, waits=len(after))
    return pl.pallas_call(
        kernel,
        grid_spec=pltpu.PrefetchScalarGridSpec(
            num_scalar_prefetch=1,
            grid=(heads, tiles),
            in_specs=[row_spec, key_spec, key_spec, row_spec, row_spec, row_spec, row_spec]
            + [pl.BlockSpec(memory_space=pl.ANY)] * len(after),
            out_specs=[row_spec, key_spec, key_spec],
            scratch_shapes=[pltpu.VMEM((block_len, DH), jnp.float32)],
        ),
        out_shape=[jax.ShapeDtypeStruct((block_len, cols), jnp.float32)] * 3,
        compiler_params=pltpu.CompilerParams(dimension_semantics=("arbitrary", "arbitrary")),
    )(flag, queries, keys, values, grads, attended32, row_max, row_total, *after)


def local(queries, keys, values, out_weight, cotangent, block_keep):
    block_len = queries.shape[0]
    local_cols = queries.shape[1]
    score_scale = 1.0 / math.sqrt(DH)
    axis_len = lax.axis_size("ctx")
    levels = axis_len.bit_length() - 1
    block_index = lax.axis_index("ctx")
    stacked = jnp.stack([keys, values])
    remote = [passed_along(stacked, "ctx", 1 << level) for level in range(levels)]
    row_pick = lax.broadcasted_iota(jnp.int32, block_keep.shape, 0) == block_index
    keep_row = jnp.sum(jnp.where(row_pick, block_keep, 0), axis=0)
    column_ids = lax.broadcasted_iota(jnp.int32, keep_row.shape, 0)
    own_flag = jnp.ones((1,), jnp.int32)
    flags = []
    for level in range(levels):
        target = block_index - (1 << level)
        linked = jnp.sum(jnp.where(column_ids == target, keep_row, 0))
        flags.append(((target >= 0) & (linked == 1)).astype(jnp.int32).reshape(1))

    tp_len = lax.axis_size("tp")
    tp_index = lax.axis_index("tp")
    weight_cols = lax.all_to_all(out_weight, "tp", split_axis=1, concat_axis=0, tiled=True)
    grad_part = lax.dot_general(
        cotangent, weight_cols, (((1,), (1,)), ((), ())), preferred_element_type=jnp.float32
    )
    grad_parts = lax.all_to_all(
        grad_part.astype(jnp.bfloat16).reshape(block_len, tp_len, local_cols), "tp", 1, 1, tiled=True
    )
    grad_heads = jnp.sum(grad_parts.astype(jnp.float32), axis=1).astype(jnp.bfloat16)

    state = forward_block(own_flag, queries, keys, values, None, True, score_scale)
    for number, level in enumerate(FORWARD_ORDER[:levels]):
        after = (grad_heads,) if number == levels - 1 else ()
        state = forward_block(
            flags[level], queries, remote[level][0], remote[level][1], state, False, score_scale, after
        )
    row_max, row_total, total = state
    attended32 = total / row_total
    attended = attended32.astype(jnp.bfloat16)
    spread = jnp.broadcast_to(attended[None], (tp_len,) + attended.shape)
    att_parts = lax.all_to_all(spread, "tp", 0, 0, tiled=True)
    mixed_sum = jnp.einsum(
        "ktc,kcf->tf",
        att_parts,
        weight_cols.reshape(tp_len, local_cols, weight_cols.shape[1]),
        preferred_element_type=jnp.float32,
    )
    mixed = mixed_sum.astype(jnp.bfloat16)
    weight_part = jnp.einsum("ktc,tf->kcf", att_parts, cotangent, preferred_element_type=jnp.float32)
    halves = cotangent.shape[1] // local_cols
    pieces = (
        weight_part.astype(jnp.bfloat16)
        .reshape(tp_len, local_cols, halves, local_cols)
        .transpose(0, 2, 1, 3)
        .reshape(tp_len * halves, local_cols, local_cols)
    )
    reduced = jnp.sum(lax.all_to_all(pieces, "ctx", 0, 0, tiled=True).astype(jnp.float32), axis=0)
    moves = []
    for k in range(axis_len):
        for p in range(tp_len):
            moves.append((k * tp_len + p, (halves * p + k % halves) * tp_len + k // halves))
    d_weight = lax.ppermute(reduced, ("ctx", "tp"), moves)
    arrived = []
    query_parts = []
    after = ()
    for level in BACKWARD_ORDER[:levels]:
        part, key_grad, value_grad = backward_block(
            flags[level], queries, remote[level][0], remote[level][1], grad_heads, attended32, row_max, row_total,
            False, score_scale, after,
        )
        query_parts.append(part)
        back = jnp.stack([key_grad, value_grad]).astype(jnp.bfloat16)
        after = (back,)
        arrived.append(passed_along(back, "ctx", -(1 << level)).astype(jnp.float32))
    part, own_key, own_value = backward_block(
        own_flag, queries, keys, values, grad_heads, attended32, row_max, row_total, True, score_scale, after
    )
    grad_query = part
    for part in query_parts:
        grad_query = grad_query + part
    for back in arrived:
        own_key = own_key + back[0]
        own_value = own_value + back[1]
    return (mixed, grad_query, own_key, own_value, d_weight)


def solution(mesh):
    in_specs = (P("ctx", "tp"), P("ctx", "tp"), P("ctx", "tp"), P("tp", None), P("ctx", "tp"), P())
    out_specs = (P("ctx", "tp"), P("ctx", "tp"), P("ctx", "tp"), P("ctx", "tp"), P("tp", "ctx"))
    return jax.shard_map(local, mesh=mesh, in_specs=in_specs, out_specs=out_specs, check_vma=False)
```

```python
import functools
import math

import jax
import jax.numpy as jnp
from jax import lax
from jax.experimental import pallas as pl
from jax.experimental.pallas import tpu as pltpu
from jax.sharding import PartitionSpec as P

DH = 128
NEG = -1e30
KEY_TILE = 512
FORWARD_ORDER = (0, 2, 1, 3)
BACKWARD_ORDER = (3, 1, 2, 0)


def passed_along(value, axis, steps):
    count = lax.axis_size(axis)
    initial, last = (max(0, -steps), min(count, count - steps))
    return lax.ppermute(value, axis, [(source, source + steps) for source in range(initial, last)])


def block_scores(q, k, tile, causal, scale):
    raw = lax.dot_general(q, k, (((1,), (1,)), ((), ())), preferred_element_type=jnp.float32) * scale
    if not causal:
        return raw
    rows = lax.broadcasted_iota(jnp.int32, raw.shape, 0)
    cols = lax.broadcasted_iota(jnp.int32, raw.shape, 1) + tile * raw.shape[1]
    return jnp.where(rows >= cols, raw, NEG)


def forward_kernel(flag_ref, *refs, causal, first, tiles, scale, waits):
    refs = refs[:3] + refs[3 + waits:]
    if first:
        q_ref, k_ref, v_ref, m_ref, l_ref, acc_ref, m_sc, l_sc, acc_sc = refs
    else:
        q_ref, k_ref, v_ref, m_in, l_in, acc_in, m_ref, l_ref, acc_ref, m_sc, l_sc, acc_sc = refs
    tile = pl.program_id(1)

    @pl.when(tile == 0)
    def _():
        if first:
            m_sc[...] = jnp.full(m_sc.shape, NEG, jnp.float32)
            l_sc[...] = jnp.zeros(l_sc.shape, jnp.float32)
            acc_sc[...] = jnp.zeros(acc_sc.shape, jnp.float32)
        else:
            m_sc[...] = m_in[:, :1]
            l_sc[...] = l_in[:, :1]
            acc_sc[...] = acc_in[...]

    @pl.when(flag_ref[0] == 1)
    def _():
        scores = block_scores(q_ref[...], k_ref[...], tile, causal, scale)
        old = m_sc[...]
        new = jnp.maximum(old, jnp.max(scores, axis=1, keepdims=True))
        alpha = jnp.exp(old - new)
        expd = jnp.exp(scores - new)
        l_sc[...] = l_sc[...] * alpha + jnp.sum(expd, axis=1, keepdims=True)
        acc_sc[...] = acc_sc[...] * alpha + jnp.dot(
            expd.astype(jnp.bfloat16), v_ref[...], preferred_element_type=jnp.float32
        )
        m_sc[...] = new

    @pl.when(tile == tiles - 1)
    def _():
        m_ref[...] = jnp.broadcast_to(m_sc[...], m_ref.shape)
        l_ref[...] = jnp.broadcast_to(l_sc[...], l_ref.shape)
        acc_ref[...] = acc_sc[...]


def forward_block(flag, queries, keys, values, state, causal, scale, after=()):
    block_len, cols = queries.shape
    heads = cols // DH
    tiles = block_len // KEY_TILE
    first = state is None
    row_spec = pl.BlockSpec((block_len, DH), lambda h, t, f: (0, h))
    key_spec = pl.BlockSpec((KEY_TILE, DH), lambda h, t, f: (t, h))
    in_specs = [row_spec, key_spec, key_spec] + [pl.BlockSpec(memory_space=pl.ANY)] * len(after)
    operands = [queries, keys, values] + list(after)
    if not first:
        in_specs += [row_spec, row_spec, row_spec]
        operands += list(state)
    kernel = functools.partial(
        forward_kernel, causal=causal, first=first, tiles=tiles, scale=scale, waits=len(after)
    )
    return pl.pallas_call(
        kernel,
        grid_spec=pltpu.PrefetchScalarGridSpec(
            num_scalar_prefetch=1,
            grid=(heads, tiles),
            in_specs=in_specs,
            out_specs=[row_spec, row_spec, row_spec],
            scratch_shapes=[
                pltpu.VMEM((block_len, 1), jnp.float32),
                pltpu.VMEM((block_len, 1), jnp.float32),
                pltpu.VMEM((block_len, DH), jnp.float32),
            ],
        ),
        out_shape=[jax.ShapeDtypeStruct((block_len, cols), jnp.float32)] * 3,
        compiler_params=pltpu.CompilerParams(dimension_semantics=("arbitrary", "arbitrary")),
    )(flag, *operands)


def backward_kernel(flag_ref, *refs, causal, tiles, scale, waits):
    refs = refs[:7] + refs[7 + waits:]
    q_ref, k_ref, v_ref, g_ref, att_ref, m_ref, l_ref, dq_ref, dk_ref, dv_ref, dq_sc = refs
    tile = pl.program_id(1)

    @pl.when(tile == 0)
    def _():
        dq_sc[...] = jnp.zeros(dq_sc.shape, jnp.float32)

    @pl.when(flag_ref[0] == 1)
    def _():
        q = q_ref[...]
        k = k_ref[...]
        g = g_ref[...]
        scores = block_scores(q, k, tile, causal, scale)
        probs = jnp.exp(scores - m_ref[:, :1]) * (1.0 / l_ref[:, :1])
        weights = probs.astype(jnp.bfloat16)
        dots = lax.dot_general(g, v_ref[...], (((1,), (1,)), ((), ())), preferred_element_type=jnp.float32)
        delta = jnp.sum(g.astype(jnp.float32) * att_ref[...], axis=1, keepdims=True)
        slopes = (probs * (dots - delta) * scale).astype(jnp.bfloat16)
        dq_sc[...] += jnp.dot(slopes, k, preferred_element_type=jnp.float32)
        dk_ref[...] = lax.dot_general(slopes, q, (((0,), (0,)), ((), ())), preferred_element_type=jnp.float32)
        dv_ref[...] = lax.dot_general(weights, g, (((0,), (0,)), ((), ())), preferred_element_type=jnp.float32)

    @pl.when(flag_ref[0] != 1)
    def _():
        dk_ref[...] = jnp.zeros(dk_ref.shape, jnp.float32)
        dv_ref[...] = jnp.zeros(dv_ref.shape, jnp.float32)

    @pl.when(tile == tiles - 1)
    def _():
        dq_ref[...] = dq_sc[...]


def backward_block(flag, queries, keys, values, grads, attended32, row_max, row_total, causal, scale, after=()):
    block_len, cols = queries.shape
    heads = cols // DH
    tiles = block_len // KEY_TILE
    row_spec = pl.BlockSpec((block_len, DH), lambda h, t, f: (0, h))
    key_spec = pl.BlockSpec((KEY_TILE, DH), lambda h, t, f: (t, h))
    kernel = functools.partial(backward_kernel, causal=causal, tiles=tiles, scale=scale, waits=len(after))
    return pl.pallas_call(
        kernel,
        grid_spec=pltpu.PrefetchScalarGridSpec(
            num_scalar_prefetch=1,
            grid=(heads, tiles),
            in_specs=[row_spec, key_spec, key_spec, row_spec, row_spec, row_spec, row_spec]
            + [pl.BlockSpec(memory_space=pl.ANY)] * len(after),
            out_specs=[row_spec, key_spec, key_spec],
            scratch_shapes=[pltpu.VMEM((block_len, DH), jnp.float32)],
        ),
        out_shape=[jax.ShapeDtypeStruct((block_len, cols), jnp.float32)] * 3,
        compiler_params=pltpu.CompilerParams(dimension_semantics=("arbitrary", "arbitrary")),
    )(flag, queries, keys, values, grads, attended32, row_max, row_total, *after)


def local(queries, keys, values, out_weight, cotangent, block_keep):
    block_len = queries.shape[0]
    local_cols = queries.shape[1]
    score_scale = 1.0 / math.sqrt(DH)
    axis_len = lax.axis_size("ctx")
    levels = axis_len.bit_length() - 1
    block_index = lax.axis_index("ctx")
    stacked = jnp.stack([keys, values])
    remote = [passed_along(stacked, "ctx", 1 << level) for level in range(levels)]
    row_pick = lax.broadcasted_iota(jnp.int32, block_keep.shape, 0) == block_index
    keep_row = jnp.sum(jnp.where(row_pick, block_keep, 0), axis=0)
    column_ids = lax.broadcasted_iota(jnp.int32, keep_row.shape, 0)
    own_flag = jnp.ones((1,), jnp.int32)
    flags = []
    for level in range(levels):
        target = block_index - (1 << level)
        linked = jnp.sum(jnp.where(column_ids == target, keep_row, 0))
        flags.append(((target >= 0) & (linked == 1)).astype(jnp.int32).reshape(1))

    tp_len = lax.axis_size("tp")
    tp_index = lax.axis_index("tp")
    width = out_weight.shape[1] // tp_len
    shares = out_weight.reshape(out_weight.shape[0], tp_len, width)
    received = [shares[:, tp_index]]
    for shift in range(1, tp_len):
        share = lax.dynamic_index_in_dim(shares, (tp_index + shift) % tp_len, axis=1, keepdims=False)
        received.append(lax.ppermute(share, "tp", [(i, (i + shift) % tp_len) for i in range(tp_len)]))
    by_shift = jnp.stack(received)
    by_source = jnp.take(by_shift, (tp_index - jnp.arange(tp_len)) % tp_len, axis=0)
    weight_cols = by_source.reshape(tp_len * out_weight.shape[0], width)
    grad_part = lax.dot_general(
        cotangent, weight_cols, (((1,), (1,)), ((), ())), preferred_element_type=jnp.float32
    )
    grad_parts = lax.all_to_all(
        grad_part.astype(jnp.bfloat16).reshape(block_len, tp_len, local_cols), "tp", 1, 1, tiled=True
    )
    grad_heads = jnp.sum(grad_parts.astype(jnp.float32), axis=1).astype(jnp.bfloat16)

    state = forward_block(own_flag, queries, keys, values, None, True, score_scale)
    for number, level in enumerate(FORWARD_ORDER[:levels]):
        after = (grad_heads,) if number == levels - 1 else ()
        state = forward_block(
            flags[level], queries, remote[level][0], remote[level][1], state, False, score_scale, after
        )
    row_max, row_total, total = state
    attended32 = total / row_total
    attended = attended32.astype(jnp.bfloat16)
    spread = jnp.broadcast_to(attended[None], (tp_len,) + attended.shape)
    att_parts = lax.all_to_all(spread, "tp", 0, 0, tiled=True)
    mixed_sum = jnp.einsum(
        "ktc,kcf->tf",
        att_parts,
        weight_cols.reshape(tp_len, local_cols, weight_cols.shape[1]),
        preferred_element_type=jnp.float32,
    )
    mixed = mixed_sum.astype(jnp.bfloat16)
    weight_part = jnp.einsum("ktc,tf->kcf", att_parts, cotangent, preferred_element_type=jnp.float32)
    halves = cotangent.shape[1] // local_cols
    pieces = (
        weight_part.astype(jnp.bfloat16)
        .reshape(tp_len, local_cols, halves, local_cols)
        .transpose(0, 2, 1, 3)
        .reshape(tp_len * halves, local_cols, local_cols)
    )
    reduced = jnp.sum(lax.all_to_all(pieces, "ctx", 0, 0, tiled=True).astype(jnp.float32), axis=0)
    moves = []
    for k in range(axis_len):
        for p in range(tp_len):
            moves.append((k * tp_len + p, (halves * p + k % halves) * tp_len + k // halves))
    d_weight = lax.ppermute(reduced, ("ctx", "tp"), moves)
    arrived = []
    query_parts = []
    after = ()
    for level in BACKWARD_ORDER[:levels]:
        part, key_grad, value_grad = backward_block(
            flags[level], queries, remote[level][0], remote[level][1], grad_heads, attended32, row_max, row_total,
            False, score_scale, after,
        )
        query_parts.append(part)
        back = jnp.stack([key_grad, value_grad]).astype(jnp.bfloat16)
        after = (back,)
        arrived.append(passed_along(back, "ctx", -(1 << level)).astype(jnp.float32))
    part, own_key, own_value = backward_block(
        own_flag, queries, keys, values, grad_heads, attended32, row_max, row_total, True, score_scale, after
    )
    grad_query = part
    for part in query_parts:
        grad_query = grad_query + part
    for back in arrived:
        own_key = own_key + back[0]
        own_value = own_value + back[1]
    return (mixed, grad_query, own_key, own_value, d_weight)


def solution(mesh):
    in_specs = (P("ctx", "tp"), P("ctx", "tp"), P("ctx", "tp"), P("tp", None), P("ctx", "tp"), P())
    out_specs = (P("ctx", "tp"), P("ctx", "tp"), P("ctx", "tp"), P("ctx", "tp"), P("tp", "ctx"))
    return jax.shard_map(local, mesh=mesh, in_specs=in_specs, out_specs=out_specs, check_vma=False)
```

```python
import functools
import math

import jax
import jax.numpy as jnp
from jax import lax
from jax.experimental import pallas as pl
from jax.experimental.pallas import tpu as pltpu
from jax.sharding import PartitionSpec as P

DH = 128
NEG = -1e30
KEY_TILE = 1024
FORWARD_ORDER = (0, 2, 1, 3)
BACKWARD_ORDER = (3, 1, 2, 0)


def passed_along(value, axis, steps):
    count = lax.axis_size(axis)
    initial, last = (max(0, -steps), min(count, count - steps))
    return lax.ppermute(value, axis, [(source, source + steps) for source in range(initial, last)])


def block_scores(q, k, tile, causal, scale):
    raw = lax.dot_general(q, k, (((1,), (1,)), ((), ())), preferred_element_type=jnp.float32) * scale
    if not causal:
        return raw
    rows = lax.broadcasted_iota(jnp.int32, raw.shape, 0)
    cols = lax.broadcasted_iota(jnp.int32, raw.shape, 1) + tile * raw.shape[1]
    return jnp.where(rows >= cols, raw, NEG)


def forward_kernel(flag_ref, *refs, causal, first, tiles, scale, waits):
    refs = refs[:3] + refs[3 + waits:]
    if first:
        q_ref, k_ref, v_ref, m_ref, l_ref, acc_ref, m_sc, l_sc, acc_sc = refs
    else:
        q_ref, k_ref, v_ref, m_in, l_in, acc_in, m_ref, l_ref, acc_ref, m_sc, l_sc, acc_sc = refs
    tile = pl.program_id(1)

    @pl.when(tile == 0)
    def _():
        if first:
            m_sc[...] = jnp.full(m_sc.shape, NEG, jnp.float32)
            l_sc[...] = jnp.zeros(l_sc.shape, jnp.float32)
            acc_sc[...] = jnp.zeros(acc_sc.shape, jnp.float32)
        else:
            m_sc[...] = m_in[:, :1]
            l_sc[...] = l_in[:, :1]
            acc_sc[...] = acc_in[...]

    @pl.when(flag_ref[0] == 1)
    def _():
        scores = block_scores(q_ref[...], k_ref[...], tile, causal, scale)
        old = m_sc[...]
        new = jnp.maximum(old, jnp.max(scores, axis=1, keepdims=True))
        alpha = jnp.exp(old - new)
        expd = jnp.exp(scores - new)
        l_sc[...] = l_sc[...] * alpha + jnp.sum(expd, axis=1, keepdims=True)
        acc_sc[...] = acc_sc[...] * alpha + jnp.dot(
            expd.astype(jnp.bfloat16), v_ref[...], preferred_element_type=jnp.float32
        )
        m_sc[...] = new

    @pl.when(tile == tiles - 1)
    def _():
        m_ref[...] = jnp.broadcast_to(m_sc[...], m_ref.shape)
        l_ref[...] = jnp.broadcast_to(l_sc[...], l_ref.shape)
        acc_ref[...] = acc_sc[...]


def forward_block(flag, queries, keys, values, state, causal, scale, after=()):
    block_len, cols = queries.shape
    heads = cols // DH
    tiles = block_len // KEY_TILE
    first = state is None
    row_spec = pl.BlockSpec((block_len, DH), lambda h, t, f: (0, h))
    key_spec = pl.BlockSpec((KEY_TILE, DH), lambda h, t, f: (t, h))
    in_specs = [row_spec, key_spec, key_spec] + [pl.BlockSpec(memory_space=pl.ANY)] * len(after)
    operands = [queries, keys, values] + list(after)
    if not first:
        in_specs += [row_spec, row_spec, row_spec]
        operands += list(state)
    kernel = functools.partial(
        forward_kernel, causal=causal, first=first, tiles=tiles, scale=scale, waits=len(after)
    )
    return pl.pallas_call(
        kernel,
        grid_spec=pltpu.PrefetchScalarGridSpec(
            num_scalar_prefetch=1,
            grid=(heads, tiles),
            in_specs=in_specs,
            out_specs=[row_spec, row_spec, row_spec],
            scratch_shapes=[
                pltpu.VMEM((block_len, 1), jnp.float32),
                pltpu.VMEM((block_len, 1), jnp.float32),
                pltpu.VMEM((block_len, DH), jnp.float32),
            ],
        ),
        out_shape=[jax.ShapeDtypeStruct((block_len, cols), jnp.float32)] * 3,
        compiler_params=pltpu.CompilerParams(dimension_semantics=("arbitrary", "arbitrary")),
    )(flag, *operands)


def backward_kernel(flag_ref, *refs, causal, tiles, scale, waits):
    refs = refs[:7] + refs[7 + waits:]
    q_ref, k_ref, v_ref, g_ref, att_ref, m_ref, l_ref, dq_ref, dk_ref, dv_ref, dq_sc = refs
    tile = pl.program_id(1)

    @pl.when(tile == 0)
    def _():
        dq_sc[...] = jnp.zeros(dq_sc.shape, jnp.float32)

    @pl.when(flag_ref[0] == 1)
    def _():
        q = q_ref[...]
        k = k_ref[...]
        g = g_ref[...]
        scores = block_scores(q, k, tile, causal, scale)
        probs = jnp.exp(scores - m_ref[:, :1]) * (1.0 / l_ref[:, :1])
        weights = probs.astype(jnp.bfloat16)
        dots = lax.dot_general(g, v_ref[...], (((1,), (1,)), ((), ())), preferred_element_type=jnp.float32)
        delta = jnp.sum(g.astype(jnp.float32) * att_ref[...], axis=1, keepdims=True)
        slopes = (probs * (dots - delta) * scale).astype(jnp.bfloat16)
        dq_sc[...] += jnp.dot(slopes, k, preferred_element_type=jnp.float32)
        dk_ref[...] = lax.dot_general(slopes, q, (((0,), (0,)), ((), ())), preferred_element_type=jnp.float32)
        dv_ref[...] = lax.dot_general(weights, g, (((0,), (0,)), ((), ())), preferred_element_type=jnp.float32)

    @pl.when(flag_ref[0] != 1)
    def _():
        dk_ref[...] = jnp.zeros(dk_ref.shape, jnp.float32)
        dv_ref[...] = jnp.zeros(dv_ref.shape, jnp.float32)

    @pl.when(tile == tiles - 1)
    def _():
        dq_ref[...] = dq_sc[...]


def backward_block(flag, queries, keys, values, grads, attended32, row_max, row_total, causal, scale, after=()):
    block_len, cols = queries.shape
    heads = cols // DH
    tiles = block_len // KEY_TILE
    row_spec = pl.BlockSpec((block_len, DH), lambda h, t, f: (0, h))
    key_spec = pl.BlockSpec((KEY_TILE, DH), lambda h, t, f: (t, h))
    kernel = functools.partial(backward_kernel, causal=causal, tiles=tiles, scale=scale, waits=len(after))
    return pl.pallas_call(
        kernel,
        grid_spec=pltpu.PrefetchScalarGridSpec(
            num_scalar_prefetch=1,
            grid=(heads, tiles),
            in_specs=[row_spec, key_spec, key_spec, row_spec, row_spec, row_spec, row_spec]
            + [pl.BlockSpec(memory_space=pl.ANY)] * len(after),
            out_specs=[row_spec, key_spec, key_spec],
            scratch_shapes=[pltpu.VMEM((block_len, DH), jnp.float32)],
        ),
        out_shape=[jax.ShapeDtypeStruct((block_len, cols), jnp.float32)] * 3,
        compiler_params=pltpu.CompilerParams(dimension_semantics=("arbitrary", "arbitrary")),
    )(flag, queries, keys, values, grads, attended32, row_max, row_total, *after)


def local(queries, keys, values, out_weight, cotangent, block_keep):
    block_len = queries.shape[0]
    local_cols = queries.shape[1]
    score_scale = 1.0 / math.sqrt(DH)
    axis_len = lax.axis_size("ctx")
    levels = axis_len.bit_length() - 1
    block_index = lax.axis_index("ctx")
    stacked = jnp.stack([keys, values])
    remote = [passed_along(stacked, "ctx", 1 << level) for level in range(levels)]
    row_pick = lax.broadcasted_iota(jnp.int32, block_keep.shape, 0) == block_index
    keep_row = jnp.sum(jnp.where(row_pick, block_keep, 0), axis=0)
    column_ids = lax.broadcasted_iota(jnp.int32, keep_row.shape, 0)
    own_flag = jnp.ones((1,), jnp.int32)
    flags = []
    for level in range(levels):
        target = block_index - (1 << level)
        linked = jnp.sum(jnp.where(column_ids == target, keep_row, 0))
        flags.append(((target >= 0) & (linked == 1)).astype(jnp.int32).reshape(1))

    tp_len = lax.axis_size("tp")
    tp_index = lax.axis_index("tp")
    weight_cols = lax.all_to_all(out_weight, "tp", split_axis=1, concat_axis=0, tiled=True)
    grad_part = lax.dot_general(
        cotangent, weight_cols, (((1,), (1,)), ((), ())), preferred_element_type=jnp.float32
    )
    grad_parts = lax.all_to_all(
        grad_part.astype(jnp.bfloat16).reshape(block_len, tp_len, local_cols), "tp", 1, 1, tiled=True
    )
    grad_heads = jnp.sum(grad_parts.astype(jnp.float32), axis=1).astype(jnp.bfloat16)

    state = forward_block(own_flag, queries, keys, values, None, True, score_scale)
    for number, level in enumerate(FORWARD_ORDER[:levels]):
        after = (grad_heads,) if number == levels - 1 else ()
        state = forward_block(
            flags[level], queries, remote[level][0], remote[level][1], state, False, score_scale, after
        )
    row_max, row_total, total = state
    attended32 = total / row_total
    attended = attended32.astype(jnp.bfloat16)
    spread = jnp.broadcast_to(attended[None], (tp_len,) + attended.shape)
    att_parts = lax.all_to_all(spread, "tp", 0, 0, tiled=True)
    mixed_sum = jnp.einsum(
        "ktc,kcf->tf",
        att_parts,
        weight_cols.reshape(tp_len, local_cols, weight_cols.shape[1]),
        preferred_element_type=jnp.float32,
    )
    mixed = mixed_sum.astype(jnp.bfloat16)
    weight_part = jnp.einsum("ktc,tf->kcf", att_parts, cotangent, preferred_element_type=jnp.float32)
    halves = cotangent.shape[1] // local_cols
    pieces = (
        weight_part.astype(jnp.bfloat16)
        .reshape(tp_len, local_cols, halves, local_cols)
        .transpose(0, 2, 1, 3)
        .reshape(tp_len * halves, local_cols, local_cols)
    )
    reduced = jnp.sum(lax.all_to_all(pieces, "ctx", 0, 0, tiled=True).astype(jnp.float32), axis=0)
    moves = []
    for k in range(axis_len):
        for p in range(tp_len):
            moves.append((k * tp_len + p, (halves * p + k % halves) * tp_len + k // halves))
    d_weight = lax.ppermute(reduced, ("ctx", "tp"), moves)
    arrived = []
    query_parts = []
    after = ()
    for level in BACKWARD_ORDER[:levels]:
        part, key_grad, value_grad = backward_block(
            flags[level], queries, remote[level][0], remote[level][1], grad_heads, attended32, row_max, row_total,
            False, score_scale, after,
        )
        query_parts.append(part)
        back = jnp.stack([key_grad, value_grad]).astype(jnp.bfloat16)
        after = (back,)
        arrived.append(passed_along(back, "ctx", -(1 << level)).astype(jnp.float32))
    part, own_key, own_value = backward_block(
        own_flag, queries, keys, values, grad_heads, attended32, row_max, row_total, True, score_scale, after
    )
    grad_query = part
    for part in query_parts:
        grad_query = grad_query + part
    for back in arrived:
        own_key = own_key + back[0]
        own_value = own_value + back[1]
    return (mixed, grad_query, own_key, own_value, d_weight)


def solution(mesh):
    in_specs = (P("ctx", "tp"), P("ctx", "tp"), P("ctx", "tp"), P("tp", None), P("ctx", "tp"), P())
    out_specs = (P("ctx", "tp"), P("ctx", "tp"), P("ctx", "tp"), P("ctx", "tp"), P("tp", "ctx"))
    return jax.shard_map(local, mesh=mesh, in_specs=in_specs, out_specs=out_specs, check_vma=False)
```

```python
import functools
import math

import jax
import jax.numpy as jnp
from jax import lax
from jax.experimental import pallas as pl
from jax.experimental.pallas import tpu as pltpu
from jax.sharding import PartitionSpec as P

DH = 128
NEG = -1e30
KEY_TILE = 1024
FORWARD_ORDER = (0, 2, 1, 3)
BACKWARD_ORDER = (3, 1, 2, 0)


def passed_along(value, axis, steps):
    count = lax.axis_size(axis)
    initial, last = (max(0, -steps), min(count, count - steps))
    return lax.ppermute(value, axis, [(source, source + steps) for source in range(initial, last)])


def block_scores(q, k, tile, causal, scale):
    raw = lax.dot_general(q, k, (((1,), (1,)), ((), ())), preferred_element_type=jnp.float32) * scale
    if not causal:
        return raw
    rows = lax.broadcasted_iota(jnp.int32, raw.shape, 0)
    cols = lax.broadcasted_iota(jnp.int32, raw.shape, 1) + tile * raw.shape[1]
    return jnp.where(rows >= cols, raw, NEG)


def forward_kernel(flag_ref, *refs, causal, first, tiles, scale, waits):
    refs = refs[:3] + refs[3 + waits:]
    if first:
        q_ref, k_ref, v_ref, m_ref, l_ref, acc_ref, m_sc, l_sc, acc_sc = refs
    else:
        q_ref, k_ref, v_ref, m_in, l_in, acc_in, m_ref, l_ref, acc_ref, m_sc, l_sc, acc_sc = refs
    tile = pl.program_id(1)

    @pl.when(tile == 0)
    def _():
        if first:
            m_sc[...] = jnp.full(m_sc.shape, NEG, jnp.float32)
            l_sc[...] = jnp.zeros(l_sc.shape, jnp.float32)
            acc_sc[...] = jnp.zeros(acc_sc.shape, jnp.float32)
        else:
            m_sc[...] = m_in[:, :1]
            l_sc[...] = l_in[:, :1]
            acc_sc[...] = acc_in[...]

    @pl.when(flag_ref[0] == 1)
    def _():
        scores = block_scores(q_ref[...], k_ref[...], tile, causal, scale)
        old = m_sc[...]
        new = jnp.maximum(old, jnp.max(scores, axis=1, keepdims=True))
        alpha = jnp.exp(old - new)
        expd = jnp.exp(scores - new)
        l_sc[...] = l_sc[...] * alpha + jnp.sum(expd, axis=1, keepdims=True)
        acc_sc[...] = acc_sc[...] * alpha + jnp.dot(
            expd.astype(jnp.bfloat16), v_ref[...], preferred_element_type=jnp.float32
        )
        m_sc[...] = new

    @pl.when(tile == tiles - 1)
    def _():
        m_ref[...] = jnp.broadcast_to(m_sc[...], m_ref.shape)
        l_ref[...] = jnp.broadcast_to(l_sc[...], l_ref.shape)
        acc_ref[...] = acc_sc[...]


def forward_block(flag, queries, keys, values, state, causal, scale, after=()):
    block_len, cols = queries.shape
    heads = cols // DH
    tiles = block_len // KEY_TILE
    first = state is None
    row_spec = pl.BlockSpec((block_len, DH), lambda h, t, f: (0, h))
    key_spec = pl.BlockSpec((KEY_TILE, DH), lambda h, t, f: (t, h))
    in_specs = [row_spec, key_spec, key_spec] + [pl.BlockSpec(memory_space=pl.ANY)] * len(after)
    operands = [queries, keys, values] + list(after)
    if not first:
        in_specs += [row_spec, row_spec, row_spec]
        operands += list(state)
    kernel = functools.partial(
        forward_kernel, causal=causal, first=first, tiles=tiles, scale=scale, waits=len(after)
    )
    return pl.pallas_call(
        kernel,
        grid_spec=pltpu.PrefetchScalarGridSpec(
            num_scalar_prefetch=1,
            grid=(heads, tiles),
            in_specs=in_specs,
            out_specs=[row_spec, row_spec, row_spec],
            scratch_shapes=[
                pltpu.VMEM((block_len, 1), jnp.float32),
                pltpu.VMEM((block_len, 1), jnp.float32),
                pltpu.VMEM((block_len, DH), jnp.float32),
            ],
        ),
        out_shape=[jax.ShapeDtypeStruct((block_len, cols), jnp.float32)] * 3,
        compiler_params=pltpu.CompilerParams(dimension_semantics=("arbitrary", "arbitrary")),
    )(flag, *operands)


def backward_kernel(flag_ref, *refs, causal, tiles, scale, waits):
    refs = refs[:7] + refs[7 + waits:]
    q_ref, k_ref, v_ref, g_ref, att_ref, m_ref, l_ref, dq_ref, dk_ref, dv_ref, dq_sc = refs
    tile = pl.program_id(1)

    @pl.when(tile == 0)
    def _():
        dq_sc[...] = jnp.zeros(dq_sc.shape, jnp.float32)

    @pl.when(flag_ref[0] == 1)
    def _():
        q = q_ref[...]
        k = k_ref[...]
        g = g_ref[...]
        scores = block_scores(q, k, tile, causal, scale)
        probs = jnp.exp(scores - m_ref[:, :1]) * (1.0 / l_ref[:, :1])
        weights = probs.astype(jnp.bfloat16)
        dots = lax.dot_general(g, v_ref[...], (((1,), (1,)), ((), ())), preferred_element_type=jnp.float32)
        delta = jnp.sum(g.astype(jnp.float32) * att_ref[...], axis=1, keepdims=True)
        slopes = (probs * (dots - delta) * scale).astype(jnp.bfloat16)
        dq_sc[...] += jnp.dot(slopes, k, preferred_element_type=jnp.float32)
        dk_ref[...] = lax.dot_general(slopes, q, (((0,), (0,)), ((), ())), preferred_element_type=jnp.float32)
        dv_ref[...] = lax.dot_general(weights, g, (((0,), (0,)), ((), ())), preferred_element_type=jnp.float32)

    @pl.when(flag_ref[0] != 1)
    def _():
        dk_ref[...] = jnp.zeros(dk_ref.shape, jnp.float32)
        dv_ref[...] = jnp.zeros(dv_ref.shape, jnp.float32)

    @pl.when(tile == tiles - 1)
    def _():
        dq_ref[...] = dq_sc[...]


def backward_block(flag, queries, keys, values, grads, attended32, row_max, row_total, causal, scale, after=()):
    block_len, cols = queries.shape
    heads = cols // DH
    tiles = block_len // KEY_TILE
    row_spec = pl.BlockSpec((block_len, DH), lambda h, t, f: (0, h))
    key_spec = pl.BlockSpec((KEY_TILE, DH), lambda h, t, f: (t, h))
    kernel = functools.partial(backward_kernel, causal=causal, tiles=tiles, scale=scale, waits=len(after))
    return pl.pallas_call(
        kernel,
        grid_spec=pltpu.PrefetchScalarGridSpec(
            num_scalar_prefetch=1,
            grid=(heads, tiles),
            in_specs=[row_spec, key_spec, key_spec, row_spec, row_spec, row_spec, row_spec]
            + [pl.BlockSpec(memory_space=pl.ANY)] * len(after),
            out_specs=[row_spec, key_spec, key_spec],
            scratch_shapes=[pltpu.VMEM((block_len, DH), jnp.float32)],
        ),
        out_shape=[jax.ShapeDtypeStruct((block_len, cols), jnp.float32)] * 3,
        compiler_params=pltpu.CompilerParams(dimension_semantics=("arbitrary", "arbitrary")),
    )(flag, queries, keys, values, grads, attended32, row_max, row_total, *after)


def local(queries, keys, values, out_weight, cotangent, block_keep):
    block_len = queries.shape[0]
    local_cols = queries.shape[1]
    score_scale = 1.0 / math.sqrt(DH)
    axis_len = lax.axis_size("ctx")
    levels = axis_len.bit_length() - 1
    block_index = lax.axis_index("ctx")
    stacked = jnp.stack([keys, values])
    remote = [passed_along(stacked, "ctx", 1 << level) for level in range(levels)]
    row_pick = lax.broadcasted_iota(jnp.int32, block_keep.shape, 0) == block_index
    keep_row = jnp.sum(jnp.where(row_pick, block_keep, 0), axis=0)
    column_ids = lax.broadcasted_iota(jnp.int32, keep_row.shape, 0)
    own_flag = jnp.ones((1,), jnp.int32)
    flags = []
    for level in range(levels):
        target = block_index - (1 << level)
        linked = jnp.sum(jnp.where(column_ids == target, keep_row, 0))
        flags.append(((target >= 0) & (linked == 1)).astype(jnp.int32).reshape(1))

    tp_len = lax.axis_size("tp")
    tp_index = lax.axis_index("tp")
    weight_cols = lax.all_to_all(out_weight, "tp", split_axis=1, concat_axis=0, tiled=True)
    grad_part = lax.dot_general(
        cotangent, weight_cols, (((1,), (1,)), ((), ())), preferred_element_type=jnp.float32
    )
    grad_parts = lax.all_to_all(
        grad_part.astype(jnp.bfloat16).reshape(block_len, tp_len, local_cols), "tp", 1, 1, tiled=True
    )
    grad_heads = jnp.sum(grad_parts.astype(jnp.float32), axis=1).astype(jnp.bfloat16)

    state = forward_block(own_flag, queries, keys, values, None, True, score_scale)
    for number, level in enumerate(FORWARD_ORDER[:levels]):
        after = (grad_heads,) if number == levels - 1 else ()
        state = forward_block(
            flags[level], queries, remote[level][0], remote[level][1], state, False, score_scale, after
        )
    row_max, row_total, total = state
    attended32 = total / row_total
    attended = attended32.astype(jnp.bfloat16)
    spread = jnp.broadcast_to(attended[None], (tp_len,) + attended.shape)
    att_parts = lax.all_to_all(spread, "tp", 0, 0, tiled=True)
    mixed_sum = jnp.einsum(
        "ktc,kcf->tf",
        att_parts,
        weight_cols.reshape(tp_len, local_cols, weight_cols.shape[1]),
        preferred_element_type=jnp.float32,
    )
    mixed = mixed_sum.astype(jnp.bfloat16)
    weight_part = jnp.einsum("ktc,tf->kcf", att_parts, cotangent, preferred_element_type=jnp.float32)
    halves = cotangent.shape[1] // local_cols
    pieces = (
        weight_part.astype(jnp.bfloat16)
        .reshape(tp_len, local_cols, halves, local_cols)
        .transpose(0, 2, 1, 3)
        .reshape(tp_len * halves, local_cols, local_cols)
    )
    reduced = jnp.sum(lax.all_to_all(pieces, "ctx", 0, 0, tiled=True).astype(jnp.float32), axis=0)
    moves = []
    for k in range(axis_len):
        for p in range(tp_len):
            moves.append((k * tp_len + p, (halves * p + k % halves) * tp_len + k // halves))
    d_weight = lax.ppermute(reduced, ("ctx", "tp"), moves)
    arrived = []
    query_parts = []
    after = ()
    for level in BACKWARD_ORDER[:levels]:
        part, key_grad, value_grad = backward_block(
            flags[level], queries, remote[level][0], remote[level][1], grad_heads, attended32, row_max, row_total,
            False, score_scale, after,
        )
        query_parts.append(part)
        back = jnp.stack([key_grad, value_grad]).astype(jnp.bfloat16)
        arrived.append(passed_along(back, "ctx", -(1 << level)))
        after = (back,) + tuple(arrived[-3:-2])
    part, own_key, own_value = backward_block(
        own_flag, queries, keys, values, grad_heads, attended32, row_max, row_total, True, score_scale, after
    )
    arrived = [back.astype(jnp.float32) for back in arrived]
    grad_query = part
    for part in query_parts:
        grad_query = grad_query + part
    for back in arrived:
        own_key = own_key + back[0]
        own_value = own_value + back[1]
    return (mixed, grad_query, own_key, own_value, d_weight)


def solution(mesh):
    in_specs = (P("ctx", "tp"), P("ctx", "tp"), P("ctx", "tp"), P("tp", None), P("ctx", "tp"), P())
    out_specs = (P("ctx", "tp"), P("ctx", "tp"), P("ctx", "tp"), P("ctx", "tp"), P("tp", "ctx"))
    return jax.shard_map(local, mesh=mesh, in_specs=in_specs, out_specs=out_specs, check_vma=False)
```

```python
import functools
import math

import jax
import jax.numpy as jnp
from jax import lax
from jax.experimental import pallas as pl
from jax.experimental.pallas import tpu as pltpu
from jax.sharding import PartitionSpec as P

DH = 128
NEG = -1e30
KEY_TILE = 1024
FORWARD_ORDER = (0, 2, 1, 3)
BACKWARD_ORDER = (3, 1, 2, 0)


def passed_along(value, axis, steps):
    count = lax.axis_size(axis)
    initial, last = (max(0, -steps), min(count, count - steps))
    return lax.ppermute(value, axis, [(source, source + steps) for source in range(initial, last)])


def block_scores(q, k, tile, causal, scale):
    raw = lax.dot_general(q, k, (((1,), (1,)), ((), ())), preferred_element_type=jnp.float32) * scale
    if not causal:
        return raw
    rows = lax.broadcasted_iota(jnp.int32, raw.shape, 0)
    cols = lax.broadcasted_iota(jnp.int32, raw.shape, 1) + tile * raw.shape[1]
    return jnp.where(rows >= cols, raw, NEG)


def forward_kernel(flag_ref, *refs, causal, first, tiles, scale, waits):
    refs = refs[:3] + refs[3 + waits:]
    if first:
        q_ref, k_ref, v_ref, m_ref, l_ref, acc_ref, m_sc, l_sc, acc_sc = refs
    else:
        q_ref, k_ref, v_ref, m_in, l_in, acc_in, m_ref, l_ref, acc_ref, m_sc, l_sc, acc_sc = refs
    tile = pl.program_id(1)

    @pl.when(tile == 0)
    def _():
        if first:
            m_sc[...] = jnp.full(m_sc.shape, NEG, jnp.float32)
            l_sc[...] = jnp.zeros(l_sc.shape, jnp.float32)
            acc_sc[...] = jnp.zeros(acc_sc.shape, jnp.float32)
        else:
            m_sc[...] = m_in[:, :1]
            l_sc[...] = l_in[:, :1]
            acc_sc[...] = acc_in[...]

    @pl.when(flag_ref[0] == 1)
    def _():
        scores = block_scores(q_ref[...], k_ref[...], tile, causal, scale)
        old = m_sc[...]
        new = jnp.maximum(old, jnp.max(scores, axis=1, keepdims=True))
        alpha = jnp.exp(old - new)
        expd = jnp.exp(scores - new)
        l_sc[...] = l_sc[...] * alpha + jnp.sum(expd, axis=1, keepdims=True)
        acc_sc[...] = acc_sc[...] * alpha + jnp.dot(
            expd.astype(jnp.bfloat16), v_ref[...], preferred_element_type=jnp.float32
        )
        m_sc[...] = new

    @pl.when(tile == tiles - 1)
    def _():
        m_ref[...] = jnp.broadcast_to(m_sc[...], m_ref.shape)
        l_ref[...] = jnp.broadcast_to(l_sc[...], l_ref.shape)
        acc_ref[...] = acc_sc[...]


def forward_block(flag, queries, keys, values, state, causal, scale, after=()):
    block_len, cols = queries.shape
    heads = cols // DH
    tiles = block_len // KEY_TILE
    first = state is None
    row_spec = pl.BlockSpec((block_len, DH), lambda h, t, f: (0, h))
    key_spec = pl.BlockSpec((KEY_TILE, DH), lambda h, t, f: (t, h))
    in_specs = [row_spec, key_spec, key_spec] + [pl.BlockSpec(memory_space=pl.ANY)] * len(after)
    operands = [queries, keys, values] + list(after)
    if not first:
        in_specs += [row_spec, row_spec, row_spec]
        operands += list(state)
    kernel = functools.partial(
        forward_kernel, causal=causal, first=first, tiles=tiles, scale=scale, waits=len(after)
    )
    return pl.pallas_call(
        kernel,
        grid_spec=pltpu.PrefetchScalarGridSpec(
            num_scalar_prefetch=1,
            grid=(heads, tiles),
            in_specs=in_specs,
            out_specs=[row_spec, row_spec, row_spec],
            scratch_shapes=[
                pltpu.VMEM((block_len, 1), jnp.float32),
                pltpu.VMEM((block_len, 1), jnp.float32),
                pltpu.VMEM((block_len, DH), jnp.float32),
            ],
        ),
        out_shape=[jax.ShapeDtypeStruct((block_len, cols), jnp.float32)] * 3,
        compiler_params=pltpu.CompilerParams(dimension_semantics=("arbitrary", "arbitrary")),
    )(flag, *operands)


def backward_kernel(flag_ref, *refs, causal, tiles, scale, waits):
    refs = refs[:7] + refs[7 + waits:]
    q_ref, k_ref, v_ref, g_ref, att_ref, m_ref, l_ref, dq_ref, dk_ref, dv_ref, dq_sc = refs
    tile = pl.program_id(1)

    @pl.when(tile == 0)
    def _():
        dq_sc[...] = jnp.zeros(dq_sc.shape, jnp.float32)

    @pl.when(flag_ref[0] == 1)
    def _():
        q = q_ref[...]
        k = k_ref[...]
        g = g_ref[...]
        scores = block_scores(q, k, tile, causal, scale)
        probs = jnp.exp(scores - m_ref[:, :1]) * (1.0 / l_ref[:, :1])
        weights = probs.astype(jnp.bfloat16)
        dots = lax.dot_general(g, v_ref[...], (((1,), (1,)), ((), ())), preferred_element_type=jnp.float32)
        delta = jnp.sum(g.astype(jnp.float32) * att_ref[...], axis=1, keepdims=True)
        slopes = (probs * (dots - delta) * scale).astype(jnp.bfloat16)
        dq_sc[...] += jnp.dot(slopes, k, preferred_element_type=jnp.float32)
        dk_ref[...] = lax.dot_general(slopes, q, (((0,), (0,)), ((), ())), preferred_element_type=jnp.float32)
        dv_ref[...] = lax.dot_general(weights, g, (((0,), (0,)), ((), ())), preferred_element_type=jnp.float32)

    @pl.when(flag_ref[0] != 1)
    def _():
        dk_ref[...] = jnp.zeros(dk_ref.shape, jnp.float32)
        dv_ref[...] = jnp.zeros(dv_ref.shape, jnp.float32)

    @pl.when(tile == tiles - 1)
    def _():
        dq_ref[...] = dq_sc[...]


def backward_block(flag, queries, keys, values, grads, attended32, row_max, row_total, causal, scale, after=()):
    block_len, cols = queries.shape
    heads = cols // DH
    tiles = block_len // KEY_TILE
    row_spec = pl.BlockSpec((block_len, DH), lambda h, t, f: (0, h))
    key_spec = pl.BlockSpec((KEY_TILE, DH), lambda h, t, f: (t, h))
    kernel = functools.partial(backward_kernel, causal=causal, tiles=tiles, scale=scale, waits=len(after))
    return pl.pallas_call(
        kernel,
        grid_spec=pltpu.PrefetchScalarGridSpec(
            num_scalar_prefetch=1,
            grid=(heads, tiles),
            in_specs=[row_spec, key_spec, key_spec, row_spec, row_spec, row_spec, row_spec]
            + [pl.BlockSpec(memory_space=pl.ANY)] * len(after),
            out_specs=[row_spec, key_spec, key_spec],
            scratch_shapes=[pltpu.VMEM((block_len, DH), jnp.float32)],
        ),
        out_shape=[jax.ShapeDtypeStruct((block_len, cols), jnp.float32)] * 3,
        compiler_params=pltpu.CompilerParams(dimension_semantics=("arbitrary", "arbitrary")),
    )(flag, queries, keys, values, grads, attended32, row_max, row_total, *after)


def local(queries, keys, values, out_weight, cotangent, block_keep):
    block_len = queries.shape[0]
    local_cols = queries.shape[1]
    score_scale = 1.0 / math.sqrt(DH)
    axis_len = lax.axis_size("ctx")
    levels = axis_len.bit_length() - 1
    block_index = lax.axis_index("ctx")
    stacked = jnp.stack([keys, values])
    remote = [passed_along(stacked, "ctx", 1 << level) for level in range(levels)]
    row_pick = lax.broadcasted_iota(jnp.int32, block_keep.shape, 0) == block_index
    keep_row = jnp.sum(jnp.where(row_pick, block_keep, 0), axis=0)
    column_ids = lax.broadcasted_iota(jnp.int32, keep_row.shape, 0)
    own_flag = jnp.ones((1,), jnp.int32)
    flags = []
    for level in range(levels):
        target = block_index - (1 << level)
        linked = jnp.sum(jnp.where(column_ids == target, keep_row, 0))
        flags.append(((target >= 0) & (linked == 1)).astype(jnp.int32).reshape(1))

    tp_len = lax.axis_size("tp")
    tp_index = lax.axis_index("tp")
    weight_cols = lax.all_to_all(out_weight, "tp", split_axis=1, concat_axis=0, tiled=True)
    state = forward_block(own_flag, queries, keys, values, None, True, score_scale)
    state, cot_after = lax.optimization_barrier((state, cotangent))
    grad_part = lax.dot_general(
        cot_after, weight_cols, (((1,), (1,)), ((), ())), preferred_element_type=jnp.float32
    )
    grad_parts = lax.all_to_all(
        grad_part.astype(jnp.bfloat16).reshape(block_len, tp_len, local_cols), "tp", 1, 1, tiled=True
    )
    grad_heads = jnp.sum(grad_parts.astype(jnp.float32), axis=1).astype(jnp.bfloat16)

    for number, level in enumerate(FORWARD_ORDER[:levels]):
        after = (grad_heads,) if number == levels - 1 else ()
        state = forward_block(
            flags[level], queries, remote[level][0], remote[level][1], state, False, score_scale, after
        )
    row_max, row_total, total = state
    attended32 = total / row_total
    attended = attended32.astype(jnp.bfloat16)
    spread = jnp.broadcast_to(attended[None], (tp_len,) + attended.shape)
    att_parts = lax.all_to_all(spread, "tp", 0, 0, tiled=True)
    mixed_sum = jnp.einsum(
        "ktc,kcf->tf",
        att_parts,
        weight_cols.reshape(tp_len, local_cols, weight_cols.shape[1]),
        preferred_element_type=jnp.float32,
    )
    mixed = mixed_sum.astype(jnp.bfloat16)
    weight_part = jnp.einsum("ktc,tf->kcf", att_parts, cotangent, preferred_element_type=jnp.float32)
    halves = cotangent.shape[1] // local_cols
    pieces = (
        weight_part.astype(jnp.bfloat16)
        .reshape(tp_len, local_cols, halves, local_cols)
        .transpose(0, 2, 1, 3)
        .reshape(tp_len * halves, local_cols, local_cols)
    )
    reduced = jnp.sum(lax.all_to_all(pieces, "ctx", 0, 0, tiled=True).astype(jnp.float32), axis=0)
    moves = []
    for k in range(axis_len):
        for p in range(tp_len):
            moves.append((k * tp_len + p, (halves * p + k % halves) * tp_len + k // halves))
    d_weight = lax.ppermute(reduced, ("ctx", "tp"), moves)
    arrived = []
    query_parts = []
    after = ()
    for level in BACKWARD_ORDER[:levels]:
        part, key_grad, value_grad = backward_block(
            flags[level], queries, remote[level][0], remote[level][1], grad_heads, attended32, row_max, row_total,
            False, score_scale, after,
        )
        query_parts.append(part)
        back = jnp.stack([key_grad, value_grad]).astype(jnp.bfloat16)
        arrived.append(passed_along(back, "ctx", -(1 << level)))
        after = (back,) + tuple(arrived[-3:-2])
    part, own_key, own_value = backward_block(
        own_flag, queries, keys, values, grad_heads, attended32, row_max, row_total, True, score_scale, after
    )
    arrived = [back.astype(jnp.float32) for back in arrived]
    grad_query = part
    for part in query_parts:
        grad_query = grad_query + part
    for back in arrived:
        own_key = own_key + back[0]
        own_value = own_value + back[1]
    return (mixed, grad_query, own_key, own_value, d_weight)


def solution(mesh):
    in_specs = (P("ctx", "tp"), P("ctx", "tp"), P("ctx", "tp"), P("tp", None), P("ctx", "tp"), P())
    out_specs = (P("ctx", "tp"), P("ctx", "tp"), P("ctx", "tp"), P("ctx", "tp"), P("tp", "ctx"))
    return jax.shard_map(local, mesh=mesh, in_specs=in_specs, out_specs=out_specs, check_vma=False)
```

```python
import functools
import math

import jax
import jax.numpy as jnp
from jax import lax
from jax.experimental import pallas as pl
from jax.experimental.pallas import tpu as pltpu
from jax.sharding import PartitionSpec as P

DH = 128
NEG = -1e30
KEY_TILE = 1024
FORWARD_ORDER = (0, 2, 1, 3)
BACKWARD_ORDER = (3, 1, 2, 0)


def passed_along(value, axis, steps):
    count = lax.axis_size(axis)
    initial, last = (max(0, -steps), min(count, count - steps))
    return lax.ppermute(value, axis, [(source, source + steps) for source in range(initial, last)])


def block_scores(q, k, tile, causal, scale):
    raw = lax.dot_general(q, k, (((1,), (1,)), ((), ())), preferred_element_type=jnp.float32) * scale
    if not causal:
        return raw
    rows = lax.broadcasted_iota(jnp.int32, raw.shape, 0)
    cols = lax.broadcasted_iota(jnp.int32, raw.shape, 1) + tile * raw.shape[1]
    return jnp.where(rows >= cols, raw, NEG)


def forward_kernel(flag_ref, *refs, causal, first, tiles, scale, waits):
    refs = refs[:3] + refs[3 + waits:]
    if first:
        q_ref, k_ref, v_ref, m_ref, l_ref, acc_ref, m_sc, l_sc, acc_sc = refs
    else:
        q_ref, k_ref, v_ref, m_in, l_in, acc_in, m_ref, l_ref, acc_ref, m_sc, l_sc, acc_sc = refs
    tile = pl.program_id(1)

    @pl.when(tile == 0)
    def _():
        if first:
            m_sc[...] = jnp.full(m_sc.shape, NEG, jnp.float32)
            l_sc[...] = jnp.zeros(l_sc.shape, jnp.float32)
            acc_sc[...] = jnp.zeros(acc_sc.shape, jnp.float32)
        else:
            m_sc[...] = m_in[:, :1]
            l_sc[...] = l_in[:, :1]
            acc_sc[...] = acc_in[...]

    @pl.when(flag_ref[0] == 1)
    def _():
        scores = block_scores(q_ref[...], k_ref[...], tile, causal, scale)
        old = m_sc[...]
        new = jnp.maximum(old, jnp.max(scores, axis=1, keepdims=True))
        alpha = jnp.exp(old - new)
        expd = jnp.exp(scores - new)
        l_sc[...] = l_sc[...] * alpha + jnp.sum(expd, axis=1, keepdims=True)
        acc_sc[...] = acc_sc[...] * alpha + jnp.dot(
            expd.astype(jnp.bfloat16), v_ref[...], preferred_element_type=jnp.float32
        )
        m_sc[...] = new

    @pl.when(tile == tiles - 1)
    def _():
        m_ref[...] = jnp.broadcast_to(m_sc[...], m_ref.shape)
        l_ref[...] = jnp.broadcast_to(l_sc[...], l_ref.shape)
        acc_ref[...] = acc_sc[...]


def forward_block(flag, queries, keys, values, state, causal, scale, after=()):
    block_len, cols = queries.shape
    heads = cols // DH
    tiles = block_len // KEY_TILE
    first = state is None
    row_spec = pl.BlockSpec((block_len, DH), lambda h, t, f: (0, h))
    key_spec = pl.BlockSpec((KEY_TILE, DH), lambda h, t, f: (t, h))
    in_specs = [row_spec, key_spec, key_spec] + [pl.BlockSpec(memory_space=pl.ANY)] * len(after)
    operands = [queries, keys, values] + list(after)
    if not first:
        in_specs += [row_spec, row_spec, row_spec]
        operands += list(state)
    kernel = functools.partial(
        forward_kernel, causal=causal, first=first, tiles=tiles, scale=scale, waits=len(after)
    )
    return pl.pallas_call(
        kernel,
        grid_spec=pltpu.PrefetchScalarGridSpec(
            num_scalar_prefetch=1,
            grid=(heads, tiles),
            in_specs=in_specs,
            out_specs=[row_spec, row_spec, row_spec],
            scratch_shapes=[
                pltpu.VMEM((block_len, 1), jnp.float32),
                pltpu.VMEM((block_len, 1), jnp.float32),
                pltpu.VMEM((block_len, DH), jnp.float32),
            ],
        ),
        out_shape=[jax.ShapeDtypeStruct((block_len, cols), jnp.float32)] * 3,
        compiler_params=pltpu.CompilerParams(dimension_semantics=("arbitrary", "arbitrary")),
    )(flag, *operands)


def backward_kernel(flag_ref, *refs, causal, tiles, scale, waits):
    refs = refs[:7] + refs[7 + waits:]
    q_ref, k_ref, v_ref, g_ref, att_ref, m_ref, l_ref, dq_ref, dk_ref, dv_ref, dq_sc = refs
    tile = pl.program_id(1)

    @pl.when(tile == 0)
    def _():
        dq_sc[...] = jnp.zeros(dq_sc.shape, jnp.float32)

    @pl.when(flag_ref[0] == 1)
    def _():
        q = q_ref[...]
        k = k_ref[...]
        g = g_ref[...]
        scores = block_scores(q, k, tile, causal, scale)
        probs = jnp.exp(scores - m_ref[:, :1]) * (1.0 / l_ref[:, :1])
        weights = probs.astype(jnp.bfloat16)
        dots = lax.dot_general(g, v_ref[...], (((1,), (1,)), ((), ())), preferred_element_type=jnp.float32)
        delta = jnp.sum(g.astype(jnp.float32) * att_ref[...], axis=1, keepdims=True)
        slopes = (probs * (dots - delta) * scale).astype(jnp.bfloat16)
        dq_sc[...] += jnp.dot(slopes, k, preferred_element_type=jnp.float32)
        dk_ref[...] = lax.dot_general(slopes, q, (((0,), (0,)), ((), ())), preferred_element_type=jnp.float32)
        dv_ref[...] = lax.dot_general(weights, g, (((0,), (0,)), ((), ())), preferred_element_type=jnp.float32)

    @pl.when(flag_ref[0] != 1)
    def _():
        dk_ref[...] = jnp.zeros(dk_ref.shape, jnp.float32)
        dv_ref[...] = jnp.zeros(dv_ref.shape, jnp.float32)

    @pl.when(tile == tiles - 1)
    def _():
        dq_ref[...] = dq_sc[...]


def backward_block(flag, queries, keys, values, grads, attended32, row_max, row_total, causal, scale, after=()):
    block_len, cols = queries.shape
    heads = cols // DH
    tiles = block_len // KEY_TILE
    row_spec = pl.BlockSpec((block_len, DH), lambda h, t, f: (0, h))
    key_spec = pl.BlockSpec((KEY_TILE, DH), lambda h, t, f: (t, h))
    kernel = functools.partial(backward_kernel, causal=causal, tiles=tiles, scale=scale, waits=len(after))
    return pl.pallas_call(
        kernel,
        grid_spec=pltpu.PrefetchScalarGridSpec(
            num_scalar_prefetch=1,
            grid=(heads, tiles),
            in_specs=[row_spec, key_spec, key_spec, row_spec, row_spec, row_spec, row_spec]
            + [pl.BlockSpec(memory_space=pl.ANY)] * len(after),
            out_specs=[row_spec, key_spec, key_spec],
            scratch_shapes=[pltpu.VMEM((block_len, DH), jnp.float32)],
        ),
        out_shape=[jax.ShapeDtypeStruct((block_len, cols), jnp.float32)] * 3,
        compiler_params=pltpu.CompilerParams(dimension_semantics=("arbitrary", "arbitrary")),
    )(flag, queries, keys, values, grads, attended32, row_max, row_total, *after)


def local(queries, keys, values, out_weight, cotangent, block_keep):
    block_len = queries.shape[0]
    local_cols = queries.shape[1]
    score_scale = 1.0 / math.sqrt(DH)
    axis_len = lax.axis_size("ctx")
    levels = axis_len.bit_length() - 1
    block_index = lax.axis_index("ctx")
    stacked = jnp.stack([keys, values])
    remote = [passed_along(stacked, "ctx", 1 << level) for level in range(levels)]
    row_pick = lax.broadcasted_iota(jnp.int32, block_keep.shape, 0) == block_index
    keep_row = jnp.sum(jnp.where(row_pick, block_keep, 0), axis=0)
    column_ids = lax.broadcasted_iota(jnp.int32, keep_row.shape, 0)
    own_flag = jnp.ones((1,), jnp.int32)
    flags = []
    for level in range(levels):
        target = block_index - (1 << level)
        linked = jnp.sum(jnp.where(column_ids == target, keep_row, 0))
        flags.append(((target >= 0) & (linked == 1)).astype(jnp.int32).reshape(1))

    tp_len = lax.axis_size("tp")
    tp_index = lax.axis_index("tp")
    weight_cols = lax.all_to_all(out_weight, "tp", split_axis=1, concat_axis=0, tiled=True)
    grad_part = lax.dot_general(
        cotangent, weight_cols, (((1,), (1,)), ((), ())), preferred_element_type=jnp.float32
    )
    grad_parts = lax.all_to_all(
        grad_part.astype(jnp.bfloat16).reshape(block_len, tp_len, local_cols), "tp", 1, 1, tiled=True
    )
    grad_heads = jnp.sum(grad_parts.astype(jnp.float32), axis=1).astype(jnp.bfloat16)

    state = forward_block(own_flag, queries, keys, values, None, True, score_scale)
    for number, level in enumerate(FORWARD_ORDER[:levels]):
        after = (grad_heads,) if number == levels - 1 else ()
        state = forward_block(
            flags[level], queries, remote[level][0], remote[level][1], state, False, score_scale, after
        )
    row_max, row_total, total = state
    attended32 = total / row_total
    attended = attended32.astype(jnp.bfloat16)
    spread = jnp.broadcast_to(attended[None], (tp_len,) + attended.shape)
    att_parts = lax.all_to_all(spread, "tp", 0, 0, tiled=True)
    mixed_sum = jnp.einsum(
        "ktc,kcf->tf",
        att_parts,
        weight_cols.reshape(tp_len, local_cols, weight_cols.shape[1]),
        preferred_element_type=jnp.float32,
    )
    mixed = mixed_sum.astype(jnp.bfloat16)
    weight_part = jnp.einsum("ktc,tf->kcf", att_parts, cotangent, preferred_element_type=jnp.float32)
    halves = cotangent.shape[1] // local_cols
    pieces = (
        weight_part.astype(jnp.bfloat16)
        .reshape(tp_len, local_cols, halves, local_cols)
        .transpose(0, 2, 1, 3)
        .reshape(tp_len * halves, local_cols, local_cols)
    )
    reduced = jnp.sum(lax.all_to_all(pieces, "ctx", 0, 0, tiled=True).astype(jnp.float32), axis=0)
    moves = []
    for k in range(axis_len):
        for p in range(tp_len):
            moves.append((k * tp_len + p, (halves * p + k % halves) * tp_len + k // halves))
    d_weight = lax.ppermute(reduced.astype(jnp.bfloat16), ("ctx", "tp"), moves).astype(jnp.float32)
    arrived = []
    query_parts = []
    after = ()
    for level in BACKWARD_ORDER[:levels]:
        part, key_grad, value_grad = backward_block(
            flags[level], queries, remote[level][0], remote[level][1], grad_heads, attended32, row_max, row_total,
            False, score_scale, after,
        )
        query_parts.append(part)
        back = jnp.stack([key_grad, value_grad]).astype(jnp.bfloat16)
        arrived.append(passed_along(back, "ctx", -(1 << level)))
        after = (back,) + tuple(arrived[-3:-2])
    part, own_key, own_value = backward_block(
        own_flag, queries, keys, values, grad_heads, attended32, row_max, row_total, True, score_scale, after
    )
    arrived = [back.astype(jnp.float32) for back in arrived]
    grad_query = part
    for part in query_parts:
        grad_query = grad_query + part
    for back in arrived:
        own_key = own_key + back[0]
        own_value = own_value + back[1]
    return (mixed, grad_query, own_key, own_value, d_weight)


def solution(mesh):
    in_specs = (P("ctx", "tp"), P("ctx", "tp"), P("ctx", "tp"), P("tp", None), P("ctx", "tp"), P())
    out_specs = (P("ctx", "tp"), P("ctx", "tp"), P("ctx", "tp"), P("ctx", "tp"), P("tp", "ctx"))
    return jax.shard_map(local, mesh=mesh, in_specs=in_specs, out_specs=out_specs, check_vma=False)
```

```python
import functools
import math

import jax
import jax.numpy as jnp
from jax import lax
from jax.experimental import pallas as pl
from jax.experimental.pallas import tpu as pltpu
from jax.sharding import PartitionSpec as P

DH = 128
NEG = -1e30
KEY_TILE = 1024
FORWARD_ORDER = (0, 2, 1, 3)
BACKWARD_ORDER = (3, 1, 2, 0)


def passed_along(value, axis, steps):
    count = lax.axis_size(axis)
    initial, last = (max(0, -steps), min(count, count - steps))
    return lax.ppermute(value, axis, [(source, source + steps) for source in range(initial, last)])


def block_scores(q, k, tile, causal, scale):
    raw = lax.dot_general(q, k, (((1,), (1,)), ((), ())), preferred_element_type=jnp.float32) * scale
    if not causal:
        return raw
    rows = lax.broadcasted_iota(jnp.int32, raw.shape, 0)
    cols = lax.broadcasted_iota(jnp.int32, raw.shape, 1) + tile * raw.shape[1]
    return jnp.where(rows >= cols, raw, NEG)


def forward_kernel(flag_ref, *refs, causal, first, tiles, scale, waits):
    refs = refs[:3] + refs[3 + waits:]
    if first:
        q_ref, k_ref, v_ref, m_ref, l_ref, acc_ref, m_sc, l_sc, acc_sc = refs
    else:
        q_ref, k_ref, v_ref, m_in, l_in, acc_in, m_ref, l_ref, acc_ref, m_sc, l_sc, acc_sc = refs
    tile = pl.program_id(1)

    @pl.when(tile == 0)
    def _():
        if first:
            m_sc[...] = jnp.full(m_sc.shape, NEG, jnp.float32)
            l_sc[...] = jnp.zeros(l_sc.shape, jnp.float32)
            acc_sc[...] = jnp.zeros(acc_sc.shape, jnp.float32)
        else:
            m_sc[...] = m_in[:, :1]
            l_sc[...] = l_in[:, :1]
            acc_sc[...] = acc_in[...]

    @pl.when(flag_ref[0] == 1)
    def _():
        scores = block_scores(q_ref[...], k_ref[...], tile, causal, scale)
        old = m_sc[...]
        new = jnp.maximum(old, jnp.max(scores, axis=1, keepdims=True))
        alpha = jnp.exp(old - new)
        expd = jnp.exp(scores - new)
        l_sc[...] = l_sc[...] * alpha + jnp.sum(expd, axis=1, keepdims=True)
        acc_sc[...] = acc_sc[...] * alpha + jnp.dot(
            expd.astype(jnp.bfloat16), v_ref[...], preferred_element_type=jnp.float32
        )
        m_sc[...] = new

    @pl.when(tile == tiles - 1)
    def _():
        m_ref[...] = jnp.broadcast_to(m_sc[...], m_ref.shape)
        l_ref[...] = jnp.broadcast_to(l_sc[...], l_ref.shape)
        acc_ref[...] = acc_sc[...]


def forward_block(flag, queries, keys, values, state, causal, scale, after=()):
    block_len, cols = queries.shape
    heads = cols // DH
    tiles = block_len // KEY_TILE
    first = state is None
    row_spec = pl.BlockSpec((block_len, DH), lambda h, t, f: (0, h))
    key_spec = pl.BlockSpec((KEY_TILE, DH), lambda h, t, f: (t, h))
    in_specs = [row_spec, key_spec, key_spec] + [pl.BlockSpec(memory_space=pl.ANY)] * len(after)
    operands = [queries, keys, values] + list(after)
    if not first:
        in_specs += [row_spec, row_spec, row_spec]
        operands += list(state)
    kernel = functools.partial(
        forward_kernel, causal=causal, first=first, tiles=tiles, scale=scale, waits=len(after)
    )
    return pl.pallas_call(
        kernel,
        grid_spec=pltpu.PrefetchScalarGridSpec(
            num_scalar_prefetch=1,
            grid=(heads, tiles),
            in_specs=in_specs,
            out_specs=[row_spec, row_spec, row_spec],
            scratch_shapes=[
                pltpu.VMEM((block_len, 1), jnp.float32),
                pltpu.VMEM((block_len, 1), jnp.float32),
                pltpu.VMEM((block_len, DH), jnp.float32),
            ],
        ),
        out_shape=[jax.ShapeDtypeStruct((block_len, cols), jnp.float32)] * 3,
        compiler_params=pltpu.CompilerParams(dimension_semantics=("arbitrary", "arbitrary")),
    )(flag, *operands)


def backward_kernel(flag_ref, *refs, causal, tiles, scale, waits):
    refs = refs[:7] + refs[7 + waits:]
    q_ref, k_ref, v_ref, g_ref, att_ref, m_ref, l_ref, dq_ref, dk_ref, dv_ref, dq_sc = refs
    tile = pl.program_id(1)

    @pl.when(tile == 0)
    def _():
        dq_sc[...] = jnp.zeros(dq_sc.shape, jnp.float32)

    @pl.when(flag_ref[0] == 1)
    def _():
        q = q_ref[...]
        k = k_ref[...]
        g = g_ref[...]
        scores = block_scores(q, k, tile, causal, scale)
        probs = jnp.exp(scores - m_ref[:, :1]) * (1.0 / l_ref[:, :1])
        weights = probs.astype(jnp.bfloat16)
        dots = lax.dot_general(g, v_ref[...], (((1,), (1,)), ((), ())), preferred_element_type=jnp.float32)
        delta = jnp.sum(g.astype(jnp.float32) * att_ref[...], axis=1, keepdims=True)
        slopes = (probs * (dots - delta) * scale).astype(jnp.bfloat16)
        dq_sc[...] += jnp.dot(slopes, k, preferred_element_type=jnp.float32)
        dk_ref[...] = lax.dot_general(slopes, q, (((0,), (0,)), ((), ())), preferred_element_type=jnp.float32)
        dv_ref[...] = lax.dot_general(weights, g, (((0,), (0,)), ((), ())), preferred_element_type=jnp.float32)

    @pl.when(flag_ref[0] != 1)
    def _():
        dk_ref[...] = jnp.zeros(dk_ref.shape, jnp.float32)
        dv_ref[...] = jnp.zeros(dv_ref.shape, jnp.float32)

    @pl.when(tile == tiles - 1)
    def _():
        dq_ref[...] = dq_sc[...]


def backward_block(flag, queries, keys, values, grads, attended32, row_max, row_total, causal, scale, after=()):
    block_len, cols = queries.shape
    heads = cols // DH
    tiles = block_len // KEY_TILE
    row_spec = pl.BlockSpec((block_len, DH), lambda h, t, f: (0, h))
    key_spec = pl.BlockSpec((KEY_TILE, DH), lambda h, t, f: (t, h))
    kernel = functools.partial(backward_kernel, causal=causal, tiles=tiles, scale=scale, waits=len(after))
    return pl.pallas_call(
        kernel,
        grid_spec=pltpu.PrefetchScalarGridSpec(
            num_scalar_prefetch=1,
            grid=(heads, tiles),
            in_specs=[row_spec, key_spec, key_spec, row_spec, row_spec, row_spec, row_spec]
            + [pl.BlockSpec(memory_space=pl.ANY)] * len(after),
            out_specs=[row_spec, key_spec, key_spec],
            scratch_shapes=[pltpu.VMEM((block_len, DH), jnp.float32)],
        ),
        out_shape=[jax.ShapeDtypeStruct((block_len, cols), jnp.float32)] * 3,
        compiler_params=pltpu.CompilerParams(dimension_semantics=("arbitrary", "arbitrary")),
    )(flag, queries, keys, values, grads, attended32, row_max, row_total, *after)


def local(queries, keys, values, out_weight, cotangent, block_keep):
    block_len = queries.shape[0]
    local_cols = queries.shape[1]
    score_scale = 1.0 / math.sqrt(DH)
    axis_len = lax.axis_size("ctx")
    levels = axis_len.bit_length() - 1
    block_index = lax.axis_index("ctx")
    stacked = jnp.stack([keys, values])
    remote = [passed_along(stacked, "ctx", 1 << level) for level in range(levels)]
    row_pick = lax.broadcasted_iota(jnp.int32, block_keep.shape, 0) == block_index
    keep_row = jnp.sum(jnp.where(row_pick, block_keep, 0), axis=0)
    column_ids = lax.broadcasted_iota(jnp.int32, keep_row.shape, 0)
    own_flag = jnp.ones((1,), jnp.int32)
    flags = []
    for level in range(levels):
        target = block_index - (1 << level)
        linked = jnp.sum(jnp.where(column_ids == target, keep_row, 0))
        flags.append(((target >= 0) & (linked == 1)).astype(jnp.int32).reshape(1))

    tp_len = lax.axis_size("tp")
    tp_index = lax.axis_index("tp")
    weight_cols = lax.all_to_all(out_weight, "tp", split_axis=1, concat_axis=0, tiled=True)
    grad_part = lax.dot_general(
        cotangent, weight_cols, (((1,), (1,)), ((), ())), preferred_element_type=jnp.float32
    )
    grad_parts = lax.all_to_all(
        grad_part.astype(jnp.bfloat16).reshape(block_len, tp_len, local_cols), "tp", 1, 1, tiled=True
    )
    grad_heads = jnp.sum(grad_parts.astype(jnp.float32), axis=1).astype(jnp.bfloat16)

    state = forward_block(own_flag, queries, keys, values, None, True, score_scale)
    for number, level in enumerate(FORWARD_ORDER[:levels]):
        after = (grad_heads,) if number == levels - 1 else ()
        state = lax.cond(
            flags[level][0] == 1,
            lambda st, kv, extra, fl=flags[level]: tuple(
                forward_block(fl, queries, kv[0], kv[1], st, False, score_scale, extra)
            ),
            lambda st, kv, extra: tuple(st),
            tuple(state), remote[level], after,
        )
    row_max, row_total, total = state
    attended32 = total / row_total
    attended = attended32.astype(jnp.bfloat16)
    spread = jnp.broadcast_to(attended[None], (tp_len,) + attended.shape)
    att_parts = lax.all_to_all(spread, "tp", 0, 0, tiled=True)
    mixed_sum = jnp.einsum(
        "ktc,kcf->tf",
        att_parts,
        weight_cols.reshape(tp_len, local_cols, weight_cols.shape[1]),
        preferred_element_type=jnp.float32,
    )
    mixed = mixed_sum.astype(jnp.bfloat16)
    weight_part = jnp.einsum("ktc,tf->kcf", att_parts, cotangent, preferred_element_type=jnp.float32)
    halves = cotangent.shape[1] // local_cols
    pieces = (
        weight_part.astype(jnp.bfloat16)
        .reshape(tp_len, local_cols, halves, local_cols)
        .transpose(0, 2, 1, 3)
        .reshape(tp_len * halves, local_cols, local_cols)
    )
    reduced = jnp.sum(lax.all_to_all(pieces, "ctx", 0, 0, tiled=True).astype(jnp.float32), axis=0)
    moves = []
    for k in range(axis_len):
        for p in range(tp_len):
            moves.append((k * tp_len + p, (halves * p + k % halves) * tp_len + k // halves))
    d_weight = lax.ppermute(reduced.astype(jnp.bfloat16), ("ctx", "tp"), moves).astype(jnp.float32)
    arrived = []
    query_parts = []
    after = ()
    for level in BACKWARD_ORDER[:levels]:
        part, key_grad, value_grad = lax.cond(
            flags[level][0] == 1,
            lambda kv, extra, fl=flags[level]: tuple(
                backward_block(
                    fl, queries, kv[0], kv[1], grad_heads, attended32, row_max, row_total, False, score_scale, extra
                )
            ),
            lambda kv, extra: (jnp.zeros_like(attended32),) * 3,
            remote[level], after,
        )
        query_parts.append(part)
        back = jnp.stack([key_grad, value_grad]).astype(jnp.bfloat16)
        arrived.append(passed_along(back, "ctx", -(1 << level)))
        after = (back,) + tuple(arrived[-3:-2])
    part, own_key, own_value = backward_block(
        own_flag, queries, keys, values, grad_heads, attended32, row_max, row_total, True, score_scale, after
    )
    arrived = [back.astype(jnp.float32) for back in arrived]
    grad_query = part
    for part in query_parts:
        grad_query = grad_query + part
    for back in arrived:
        own_key = own_key + back[0]
        own_value = own_value + back[1]
    return (mixed, grad_query, own_key, own_value, d_weight)


def solution(mesh):
    in_specs = (P("ctx", "tp"), P("ctx", "tp"), P("ctx", "tp"), P("tp", None), P("ctx", "tp"), P())
    out_specs = (P("ctx", "tp"), P("ctx", "tp"), P("ctx", "tp"), P("ctx", "tp"), P("tp", "ctx"))
    return jax.shard_map(local, mesh=mesh, in_specs=in_specs, out_specs=out_specs, check_vma=False)
```

```python
import functools
import math

import jax
import jax.numpy as jnp
from jax import lax
from jax.experimental import pallas as pl
from jax.experimental.pallas import tpu as pltpu
from jax.sharding import PartitionSpec as P

DH = 128
NEG = -1e30
KEY_TILE = 1024
FORWARD_ORDER = (0, 2, 1, 3)
BACKWARD_ORDER = (3, 1, 2, 0)


def passed_along(value, axis, steps):
    count = lax.axis_size(axis)
    initial, last = (max(0, -steps), min(count, count - steps))
    return lax.ppermute(value, axis, [(source, source + steps) for source in range(initial, last)])


def block_scores(q, k, tile, causal, scale):
    raw = lax.dot_general(q, k, (((1,), (1,)), ((), ())), preferred_element_type=jnp.float32) * scale
    if not causal:
        return raw
    rows = lax.broadcasted_iota(jnp.int32, raw.shape, 0)
    cols = lax.broadcasted_iota(jnp.int32, raw.shape, 1) + tile * raw.shape[1]
    return jnp.where(rows >= cols, raw, NEG)


def forward_kernel(flag_ref, *refs, causal, first, tiles, scale, waits):
    refs = refs[:3] + refs[3 + waits:]
    if first:
        q_ref, k_ref, v_ref, stats_ref, acc_ref, m_sc, l_sc, acc_sc = refs
    else:
        q_ref, k_ref, v_ref, stats_in, acc_in, stats_ref, acc_ref, m_sc, l_sc, acc_sc = refs
    tile = pl.program_id(1)

    @pl.when(tile == 0)
    def _():
        if first:
            m_sc[...] = jnp.full(m_sc.shape, NEG, jnp.float32)
            l_sc[...] = jnp.zeros(l_sc.shape, jnp.float32)
            acc_sc[...] = jnp.zeros(acc_sc.shape, jnp.float32)
        else:
            m_sc[...] = stats_in[:, 0:1]
            l_sc[...] = stats_in[:, 1:2]
            acc_sc[...] = acc_in[...]

    @pl.when(flag_ref[0] == 1)
    def _():
        scores = block_scores(q_ref[...], k_ref[...], tile, causal, scale)
        old = m_sc[...]
        new = jnp.maximum(old, jnp.max(scores, axis=1, keepdims=True))
        alpha = jnp.exp(old - new)
        expd = jnp.exp(scores - new)
        l_sc[...] = l_sc[...] * alpha + jnp.sum(expd, axis=1, keepdims=True)
        acc_sc[...] = acc_sc[...] * alpha + jnp.dot(
            expd.astype(jnp.bfloat16), v_ref[...], preferred_element_type=jnp.float32
        )
        m_sc[...] = new

    @pl.when(tile == tiles - 1)
    def _():
        lane = lax.broadcasted_iota(jnp.int32, stats_ref.shape, 1)
        stats_ref[...] = jnp.where(lane == 0, m_sc[...], l_sc[...])
        acc_ref[...] = acc_sc[...]


def forward_block(flag, queries, keys, values, state, causal, scale, after=()):
    block_len, cols = queries.shape
    heads = cols // DH
    tiles = block_len // KEY_TILE
    first = state is None
    row_spec = pl.BlockSpec((block_len, DH), lambda h, t, f: (0, h))
    key_spec = pl.BlockSpec((KEY_TILE, DH), lambda h, t, f: (t, h))
    in_specs = [row_spec, key_spec, key_spec] + [pl.BlockSpec(memory_space=pl.ANY)] * len(after)
    operands = [queries, keys, values] + list(after)
    if not first:
        in_specs += [row_spec, row_spec]
        operands += list(state)
    kernel = functools.partial(
        forward_kernel, causal=causal, first=first, tiles=tiles, scale=scale, waits=len(after)
    )
    return pl.pallas_call(
        kernel,
        grid_spec=pltpu.PrefetchScalarGridSpec(
            num_scalar_prefetch=1,
            grid=(heads, tiles),
            in_specs=in_specs,
            out_specs=[row_spec, row_spec],
            scratch_shapes=[
                pltpu.VMEM((block_len, 1), jnp.float32),
                pltpu.VMEM((block_len, 1), jnp.float32),
                pltpu.VMEM((block_len, DH), jnp.float32),
            ],
        ),
        out_shape=[jax.ShapeDtypeStruct((block_len, cols), jnp.float32)] * 2,
        compiler_params=pltpu.CompilerParams(dimension_semantics=("arbitrary", "arbitrary")),
    )(flag, *operands)


def backward_kernel(flag_ref, *refs, causal, tiles, scale, waits):
    refs = refs[:6] + refs[6 + waits:]
    q_ref, k_ref, v_ref, g_ref, att_ref, stats_ref, dq_ref, dk_ref, dv_ref, dq_sc = refs
    tile = pl.program_id(1)

    @pl.when(tile == 0)
    def _():
        dq_sc[...] = jnp.zeros(dq_sc.shape, jnp.float32)

    @pl.when(flag_ref[0] == 1)
    def _():
        q = q_ref[...]
        k = k_ref[...]
        g = g_ref[...]
        scores = block_scores(q, k, tile, causal, scale)
        probs = jnp.exp(scores - stats_ref[:, 0:1]) * (1.0 / stats_ref[:, 1:2])
        weights = probs.astype(jnp.bfloat16)
        dots = lax.dot_general(g, v_ref[...], (((1,), (1,)), ((), ())), preferred_element_type=jnp.float32)
        delta = jnp.sum(g.astype(jnp.float32) * att_ref[...], axis=1, keepdims=True)
        slopes = (probs * (dots - delta) * scale).astype(jnp.bfloat16)
        dq_sc[...] += jnp.dot(slopes, k, preferred_element_type=jnp.float32)
        dk_ref[...] = lax.dot_general(slopes, q, (((0,), (0,)), ((), ())), preferred_element_type=jnp.float32)
        dv_ref[...] = lax.dot_general(weights, g, (((0,), (0,)), ((), ())), preferred_element_type=jnp.float32)

    @pl.when(flag_ref[0] != 1)
    def _():
        dk_ref[...] = jnp.zeros(dk_ref.shape, jnp.float32)
        dv_ref[...] = jnp.zeros(dv_ref.shape, jnp.float32)

    @pl.when(tile == tiles - 1)
    def _():
        dq_ref[...] = dq_sc[...]


def backward_block(flag, queries, keys, values, grads, attended32, stats, causal, scale, after=()):
    block_len, cols = queries.shape
    heads = cols // DH
    tiles = block_len // KEY_TILE
    row_spec = pl.BlockSpec((block_len, DH), lambda h, t, f: (0, h))
    key_spec = pl.BlockSpec((KEY_TILE, DH), lambda h, t, f: (t, h))
    kernel = functools.partial(backward_kernel, causal=causal, tiles=tiles, scale=scale, waits=len(after))
    return pl.pallas_call(
        kernel,
        grid_spec=pltpu.PrefetchScalarGridSpec(
            num_scalar_prefetch=1,
            grid=(heads, tiles),
            in_specs=[row_spec, key_spec, key_spec, row_spec, row_spec, row_spec]
            + [pl.BlockSpec(memory_space=pl.ANY)] * len(after),
            out_specs=[row_spec, key_spec, key_spec],
            scratch_shapes=[pltpu.VMEM((block_len, DH), jnp.float32)],
        ),
        out_shape=[jax.ShapeDtypeStruct((block_len, cols), jnp.float32)] * 3,
        compiler_params=pltpu.CompilerParams(dimension_semantics=("arbitrary", "arbitrary")),
    )(flag, queries, keys, values, grads, attended32, stats, *after)


def local(queries, keys, values, out_weight, cotangent, block_keep):
    block_len = queries.shape[0]
    local_cols = queries.shape[1]
    score_scale = 1.0 / math.sqrt(DH)
    axis_len = lax.axis_size("ctx")
    levels = axis_len.bit_length() - 1
    block_index = lax.axis_index("ctx")
    stacked = jnp.stack([keys, values])
    remote = [passed_along(stacked, "ctx", 1 << level) for level in range(levels)]
    row_pick = lax.broadcasted_iota(jnp.int32, block_keep.shape, 0) == block_index
    keep_row = jnp.sum(jnp.where(row_pick, block_keep, 0), axis=0)
    column_ids = lax.broadcasted_iota(jnp.int32, keep_row.shape, 0)
    own_flag = jnp.ones((1,), jnp.int32)
    flags = []
    for level in range(levels):
        target = block_index - (1 << level)
        linked = jnp.sum(jnp.where(column_ids == target, keep_row, 0))
        flags.append(((target >= 0) & (linked == 1)).astype(jnp.int32).reshape(1))

    tp_len = lax.axis_size("tp")
    tp_index = lax.axis_index("tp")
    weight_cols = lax.all_to_all(out_weight, "tp", split_axis=1, concat_axis=0, tiled=True)
    grad_part = lax.dot_general(
        cotangent, weight_cols, (((1,), (1,)), ((), ())), preferred_element_type=jnp.float32
    )
    grad_parts = lax.all_to_all(
        grad_part.astype(jnp.bfloat16).reshape(block_len, tp_len, local_cols), "tp", 1, 1, tiled=True
    )
    grad_heads = jnp.sum(grad_parts.astype(jnp.float32), axis=1).astype(jnp.bfloat16)

    state = forward_block(own_flag, queries, keys, values, None, True, score_scale)
    for number, level in enumerate(FORWARD_ORDER[:levels]):
        after = (grad_heads,) if number == levels - 1 else ()
        state = forward_block(
            flags[level], queries, remote[level][0], remote[level][1], state, False, score_scale, after
        )
    stats, total = state
    heads = local_cols // DH
    row_total = jnp.broadcast_to(stats.reshape(block_len, heads, DH)[:, :, 1:2], (block_len, heads, DH))
    attended32 = total / row_total.reshape(block_len, local_cols)
    attended = attended32.astype(jnp.bfloat16)
    spread = jnp.broadcast_to(attended[None], (tp_len,) + attended.shape)
    att_parts = lax.all_to_all(spread, "tp", 0, 0, tiled=True)
    mixed_sum = jnp.einsum(
        "ktc,kcf->tf",
        att_parts,
        weight_cols.reshape(tp_len, local_cols, weight_cols.shape[1]),
        preferred_element_type=jnp.float32,
    )
    mixed = mixed_sum.astype(jnp.bfloat16)
    weight_part = jnp.einsum("ktc,tf->kcf", att_parts, cotangent, preferred_element_type=jnp.float32)
    halves = cotangent.shape[1] // local_cols
    pieces = (
        weight_part.astype(jnp.bfloat16)
        .reshape(tp_len, local_cols, halves, local_cols)
        .transpose(0, 2, 1, 3)
        .reshape(tp_len * halves, local_cols, local_cols)
    )
    reduced = jnp.sum(lax.all_to_all(pieces, "ctx", 0, 0, tiled=True).astype(jnp.float32), axis=0)
    moves = []
    for k in range(axis_len):
        for p in range(tp_len):
            moves.append((k * tp_len + p, (halves * p + k % halves) * tp_len + k // halves))
    d_weight = lax.ppermute(reduced.astype(jnp.bfloat16), ("ctx", "tp"), moves).astype(jnp.float32)
    arrived = []
    query_parts = []
    after = ()
    for level in BACKWARD_ORDER[:levels]:
        part, key_grad, value_grad = backward_block(
            flags[level], queries, remote[level][0], remote[level][1], grad_heads, attended32, stats,
            False, score_scale, after,
        )
        query_parts.append(part)
        back = jnp.stack([key_grad, value_grad]).astype(jnp.bfloat16)
        arrived.append(passed_along(back, "ctx", -(1 << level)))
        after = (back,) + tuple(arrived[-3:-2])
    part, own_key, own_value = backward_block(
        own_flag, queries, keys, values, grad_heads, attended32, stats, True, score_scale, after
    )
    arrived = [back.astype(jnp.float32) for back in arrived]
    grad_query = part
    for part in query_parts:
        grad_query = grad_query + part
    for back in arrived:
        own_key = own_key + back[0]
        own_value = own_value + back[1]
    return (mixed, grad_query, own_key, own_value, d_weight)


def solution(mesh):
    in_specs = (P("ctx", "tp"), P("ctx", "tp"), P("ctx", "tp"), P("tp", None), P("ctx", "tp"), P())
    out_specs = (P("ctx", "tp"), P("ctx", "tp"), P("ctx", "tp"), P("ctx", "tp"), P("tp", "ctx"))
    return jax.shard_map(local, mesh=mesh, in_specs=in_specs, out_specs=out_specs, check_vma=False)
```

```python
import functools
import math

import jax
import jax.numpy as jnp
from jax import lax
from jax.experimental import pallas as pl
from jax.experimental.pallas import tpu as pltpu
from jax.sharding import PartitionSpec as P

DH = 128
NEG = -1e30
KEY_TILE = 1024
FORWARD_ORDER = (0, 2, 1, 3)
BACKWARD_ORDER = (1, 3, 2, 0)


def passed_along(value, axis, steps):
    count = lax.axis_size(axis)
    initial, last = (max(0, -steps), min(count, count - steps))
    return lax.ppermute(value, axis, [(source, source + steps) for source in range(initial, last)])


def block_scores(q, k, tile, causal, scale):
    raw = lax.dot_general(q, k, (((1,), (1,)), ((), ())), preferred_element_type=jnp.float32) * scale
    if not causal:
        return raw
    rows = lax.broadcasted_iota(jnp.int32, raw.shape, 0)
    cols = lax.broadcasted_iota(jnp.int32, raw.shape, 1) + tile * raw.shape[1]
    return jnp.where(rows >= cols, raw, NEG)


def forward_kernel(flag_ref, *refs, causal, first, tiles, scale, waits):
    refs = refs[:3] + refs[3 + waits:]
    if first:
        q_ref, k_ref, v_ref, m_ref, l_ref, acc_ref, m_sc, l_sc, acc_sc = refs
    else:
        q_ref, k_ref, v_ref, m_in, l_in, acc_in, m_ref, l_ref, acc_ref, m_sc, l_sc, acc_sc = refs
    tile = pl.program_id(1)

    @pl.when(tile == 0)
    def _():
        if first:
            m_sc[...] = jnp.full(m_sc.shape, NEG, jnp.float32)
            l_sc[...] = jnp.zeros(l_sc.shape, jnp.float32)
            acc_sc[...] = jnp.zeros(acc_sc.shape, jnp.float32)
        else:
            m_sc[...] = m_in[:, :1]
            l_sc[...] = l_in[:, :1]
            acc_sc[...] = acc_in[...]

    @pl.when(flag_ref[0] == 1)
    def _():
        scores = block_scores(q_ref[...], k_ref[...], tile, causal, scale)
        old = m_sc[...]
        new = jnp.maximum(old, jnp.max(scores, axis=1, keepdims=True))
        alpha = jnp.exp(old - new)
        expd = jnp.exp(scores - new)
        l_sc[...] = l_sc[...] * alpha + jnp.sum(expd, axis=1, keepdims=True)
        acc_sc[...] = acc_sc[...] * alpha + jnp.dot(
            expd.astype(jnp.bfloat16), v_ref[...], preferred_element_type=jnp.float32
        )
        m_sc[...] = new

    @pl.when(tile == tiles - 1)
    def _():
        m_ref[...] = jnp.broadcast_to(m_sc[...], m_ref.shape)
        l_ref[...] = jnp.broadcast_to(l_sc[...], l_ref.shape)
        acc_ref[...] = acc_sc[...]


def forward_block(flag, queries, keys, values, state, causal, scale, after=()):
    block_len, cols = queries.shape
    heads = cols // DH
    tiles = block_len // KEY_TILE
    first = state is None
    row_spec = pl.BlockSpec((block_len, DH), lambda h, t, f: (0, h))
    key_spec = pl.BlockSpec((KEY_TILE, DH), lambda h, t, f: (t, h))
    in_specs = [row_spec, key_spec, key_spec] + [pl.BlockSpec(memory_space=pl.ANY)] * len(after)
    operands = [queries, keys, values] + list(after)
    if not first:
        in_specs += [row_spec, row_spec, row_spec]
        operands += list(state)
    kernel = functools.partial(
        forward_kernel, causal=causal, first=first, tiles=tiles, scale=scale, waits=len(after)
    )
    return pl.pallas_call(
        kernel,
        grid_spec=pltpu.PrefetchScalarGridSpec(
            num_scalar_prefetch=1,
            grid=(heads, tiles),
            in_specs=in_specs,
            out_specs=[row_spec, row_spec, row_spec],
            scratch_shapes=[
                pltpu.VMEM((block_len, 1), jnp.float32),
                pltpu.VMEM((block_len, 1), jnp.float32),
                pltpu.VMEM((block_len, DH), jnp.float32),
            ],
        ),
        out_shape=[jax.ShapeDtypeStruct((block_len, cols), jnp.float32)] * 3,
        compiler_params=pltpu.CompilerParams(dimension_semantics=("arbitrary", "arbitrary")),
    )(flag, *operands)


def backward_kernel(flag_ref, *refs, causal, tiles, scale, waits):
    refs = refs[:7] + refs[7 + waits:]
    q_ref, k_ref, v_ref, g_ref, att_ref, m_ref, l_ref, dq_ref, dk_ref, dv_ref, dq_sc = refs
    tile = pl.program_id(1)

    @pl.when(tile == 0)
    def _():
        dq_sc[...] = jnp.zeros(dq_sc.shape, jnp.float32)

    @pl.when(flag_ref[0] == 1)
    def _():
        q = q_ref[...]
        k = k_ref[...]
        g = g_ref[...]
        scores = block_scores(q, k, tile, causal, scale)
        probs = jnp.exp(scores - m_ref[:, :1]) * (1.0 / l_ref[:, :1])
        weights = probs.astype(jnp.bfloat16)
        dots = lax.dot_general(g, v_ref[...], (((1,), (1,)), ((), ())), preferred_element_type=jnp.float32)
        delta = jnp.sum(g.astype(jnp.float32) * att_ref[...], axis=1, keepdims=True)
        slopes = (probs * (dots - delta) * scale).astype(jnp.bfloat16)
        dq_sc[...] += jnp.dot(slopes, k, preferred_element_type=jnp.float32)
        dk_ref[...] = lax.dot_general(slopes, q, (((0,), (0,)), ((), ())), preferred_element_type=jnp.float32)
        dv_ref[...] = lax.dot_general(weights, g, (((0,), (0,)), ((), ())), preferred_element_type=jnp.float32)

    @pl.when(flag_ref[0] != 1)
    def _():
        dk_ref[...] = jnp.zeros(dk_ref.shape, jnp.float32)
        dv_ref[...] = jnp.zeros(dv_ref.shape, jnp.float32)

    @pl.when(tile == tiles - 1)
    def _():
        dq_ref[...] = dq_sc[...]


def backward_block(flag, queries, keys, values, grads, attended32, row_max, row_total, causal, scale, after=()):
    block_len, cols = queries.shape
    heads = cols // DH
    tiles = block_len // KEY_TILE
    row_spec = pl.BlockSpec((block_len, DH), lambda h, t, f: (0, h))
    key_spec = pl.BlockSpec((KEY_TILE, DH), lambda h, t, f: (t, h))
    kernel = functools.partial(backward_kernel, causal=causal, tiles=tiles, scale=scale, waits=len(after))
    return pl.pallas_call(
        kernel,
        grid_spec=pltpu.PrefetchScalarGridSpec(
            num_scalar_prefetch=1,
            grid=(heads, tiles),
            in_specs=[row_spec, key_spec, key_spec, row_spec, row_spec, row_spec, row_spec]
            + [pl.BlockSpec(memory_space=pl.ANY)] * len(after),
            out_specs=[row_spec, key_spec, key_spec],
            scratch_shapes=[pltpu.VMEM((block_len, DH), jnp.float32)],
        ),
        out_shape=[jax.ShapeDtypeStruct((block_len, cols), jnp.float32)] * 3,
        compiler_params=pltpu.CompilerParams(dimension_semantics=("arbitrary", "arbitrary")),
    )(flag, queries, keys, values, grads, attended32, row_max, row_total, *after)


def local(queries, keys, values, out_weight, cotangent, block_keep):
    block_len = queries.shape[0]
    local_cols = queries.shape[1]
    score_scale = 1.0 / math.sqrt(DH)
    axis_len = lax.axis_size("ctx")
    levels = axis_len.bit_length() - 1
    block_index = lax.axis_index("ctx")
    stacked = jnp.stack([keys, values])
    remote = [passed_along(stacked, "ctx", 1 << level) for level in range(levels)]
    row_pick = lax.broadcasted_iota(jnp.int32, block_keep.shape, 0) == block_index
    keep_row = jnp.sum(jnp.where(row_pick, block_keep, 0), axis=0)
    column_ids = lax.broadcasted_iota(jnp.int32, keep_row.shape, 0)
    own_flag = jnp.ones((1,), jnp.int32)
    flags = []
    for level in range(levels):
        target = block_index - (1 << level)
        linked = jnp.sum(jnp.where(column_ids == target, keep_row, 0))
        flags.append(((target >= 0) & (linked == 1)).astype(jnp.int32).reshape(1))

    tp_len = lax.axis_size("tp")
    tp_index = lax.axis_index("tp")
    weight_cols = lax.all_to_all(out_weight, "tp", split_axis=1, concat_axis=0, tiled=True)
    grad_part = lax.dot_general(
        cotangent, weight_cols, (((1,), (1,)), ((), ())), preferred_element_type=jnp.float32
    )
    grad_parts = lax.all_to_all(
        grad_part.astype(jnp.bfloat16).reshape(block_len, tp_len, local_cols), "tp", 1, 1, tiled=True
    )
    grad_heads = jnp.sum(grad_parts.astype(jnp.float32), axis=1).astype(jnp.bfloat16)

    state = forward_block(own_flag, queries, keys, values, None, True, score_scale)
    for number, level in enumerate(FORWARD_ORDER[:levels]):
        after = (grad_heads,) if number == levels - 1 else ()
        state = forward_block(
            flags[level], queries, remote[level][0], remote[level][1], state, False, score_scale, after
        )
    row_max, row_total, total = state
    attended32 = total / row_total
    attended = attended32.astype(jnp.bfloat16)
    spread = jnp.broadcast_to(attended[None], (tp_len,) + attended.shape)
    att_parts = lax.all_to_all(spread, "tp", 0, 0, tiled=True)
    mixed_sum = jnp.einsum(
        "ktc,kcf->tf",
        att_parts,
        weight_cols.reshape(tp_len, local_cols, weight_cols.shape[1]),
        preferred_element_type=jnp.float32,
    )
    mixed = mixed_sum.astype(jnp.bfloat16)
    weight_part = jnp.einsum("ktc,tf->kcf", att_parts, cotangent, preferred_element_type=jnp.float32)
    halves = cotangent.shape[1] // local_cols
    pieces = (
        weight_part.astype(jnp.bfloat16)
        .reshape(tp_len, local_cols, halves, local_cols)
        .transpose(0, 2, 1, 3)
        .reshape(tp_len * halves, local_cols, local_cols)
    )
    reduced = jnp.sum(lax.all_to_all(pieces, "ctx", 0, 0, tiled=True).astype(jnp.float32), axis=0)
    moves = []
    for k in range(axis_len):
        for p in range(tp_len):
            moves.append((k * tp_len + p, (halves * p + k % halves) * tp_len + k // halves))
    d_weight = lax.ppermute(reduced.astype(jnp.bfloat16), ("ctx", "tp"), moves).astype(jnp.float32)
    arrived = []
    query_parts = []
    after = ()
    for level in BACKWARD_ORDER[:levels]:
        part, key_grad, value_grad = backward_block(
            flags[level], queries, remote[level][0], remote[level][1], grad_heads, attended32, row_max, row_total,
            False, score_scale, after,
        )
        query_parts.append(part)
        back = jnp.stack([key_grad, value_grad]).astype(jnp.bfloat16)
        arrived.append(passed_along(back, "ctx", -(1 << level)))
        after = (back,) + tuple(arrived[-3:-2])
    part, own_key, own_value = backward_block(
        own_flag, queries, keys, values, grad_heads, attended32, row_max, row_total, True, score_scale, after
    )
    arrived = [back.astype(jnp.float32) for back in arrived]
    grad_query = part
    for part in query_parts:
        grad_query = grad_query + part
    for back in arrived:
        own_key = own_key + back[0]
        own_value = own_value + back[1]
    return (mixed, grad_query, own_key, own_value, d_weight)


def solution(mesh):
    in_specs = (P("ctx", "tp"), P("ctx", "tp"), P("ctx", "tp"), P("tp", None), P("ctx", "tp"), P())
    out_specs = (P("ctx", "tp"), P("ctx", "tp"), P("ctx", "tp"), P("ctx", "tp"), P("tp", "ctx"))
    return jax.shard_map(local, mesh=mesh, in_specs=in_specs, out_specs=out_specs, check_vma=False)
```

```python
import functools
import math

import jax
import jax.numpy as jnp
from jax import lax
from jax.experimental import pallas as pl
from jax.experimental.pallas import tpu as pltpu
from jax.sharding import PartitionSpec as P

DH = 128
NEG = -1e30
KEY_TILE = 1024
FORWARD_ORDER = (2, 0, 1, 3)
BACKWARD_ORDER = (3, 1, 2, 0)


def passed_along(value, axis, steps):
    count = lax.axis_size(axis)
    initial, last = (max(0, -steps), min(count, count - steps))
    return lax.ppermute(value, axis, [(source, source + steps) for source in range(initial, last)])


def block_scores(q, k, tile, causal, scale):
    raw = lax.dot_general(q, k, (((1,), (1,)), ((), ())), preferred_element_type=jnp.float32) * scale
    if not causal:
        return raw
    rows = lax.broadcasted_iota(jnp.int32, raw.shape, 0)
    cols = lax.broadcasted_iota(jnp.int32, raw.shape, 1) + tile * raw.shape[1]
    return jnp.where(rows >= cols, raw, NEG)


def forward_kernel(flag_ref, *refs, causal, first, tiles, scale, waits):
    refs = refs[:3] + refs[3 + waits:]
    if first:
        q_ref, k_ref, v_ref, m_ref, l_ref, acc_ref, m_sc, l_sc, acc_sc = refs
    else:
        q_ref, k_ref, v_ref, m_in, l_in, acc_in, m_ref, l_ref, acc_ref, m_sc, l_sc, acc_sc = refs
    tile = pl.program_id(1)

    @pl.when(tile == 0)
    def _():
        if first:
            m_sc[...] = jnp.full(m_sc.shape, NEG, jnp.float32)
            l_sc[...] = jnp.zeros(l_sc.shape, jnp.float32)
            acc_sc[...] = jnp.zeros(acc_sc.shape, jnp.float32)
        else:
            m_sc[...] = m_in[:, :1]
            l_sc[...] = l_in[:, :1]
            acc_sc[...] = acc_in[...]

    @pl.when(flag_ref[0] == 1)
    def _():
        scores = block_scores(q_ref[...], k_ref[...], tile, causal, scale)
        old = m_sc[...]
        new = jnp.maximum(old, jnp.max(scores, axis=1, keepdims=True))
        alpha = jnp.exp(old - new)
        expd = jnp.exp(scores - new)
        l_sc[...] = l_sc[...] * alpha + jnp.sum(expd, axis=1, keepdims=True)
        acc_sc[...] = acc_sc[...] * alpha + jnp.dot(
            expd.astype(jnp.bfloat16), v_ref[...], preferred_element_type=jnp.float32
        )
        m_sc[...] = new

    @pl.when(tile == tiles - 1)
    def _():
        m_ref[...] = jnp.broadcast_to(m_sc[...], m_ref.shape)
        l_ref[...] = jnp.broadcast_to(l_sc[...], l_ref.shape)
        acc_ref[...] = acc_sc[...]


def forward_block(flag, queries, keys, values, state, causal, scale, after=()):
    block_len, cols = queries.shape
    heads = cols // DH
    tiles = block_len // KEY_TILE
    first = state is None
    row_spec = pl.BlockSpec((block_len, DH), lambda h, t, f: (0, h))
    key_spec = pl.BlockSpec((KEY_TILE, DH), lambda h, t, f: (t, h))
    in_specs = [row_spec, key_spec, key_spec] + [pl.BlockSpec(memory_space=pl.ANY)] * len(after)
    operands = [queries, keys, values] + list(after)
    if not first:
        in_specs += [row_spec, row_spec, row_spec]
        operands += list(state)
    kernel = functools.partial(
        forward_kernel, causal=causal, first=first, tiles=tiles, scale=scale, waits=len(after)
    )
    return pl.pallas_call(
        kernel,
        grid_spec=pltpu.PrefetchScalarGridSpec(
            num_scalar_prefetch=1,
            grid=(heads, tiles),
            in_specs=in_specs,
            out_specs=[row_spec, row_spec, row_spec],
            scratch_shapes=[
                pltpu.VMEM((block_len, 1), jnp.float32),
                pltpu.VMEM((block_len, 1), jnp.float32),
                pltpu.VMEM((block_len, DH), jnp.float32),
            ],
        ),
        out_shape=[jax.ShapeDtypeStruct((block_len, cols), jnp.float32)] * 3,
        compiler_params=pltpu.CompilerParams(dimension_semantics=("arbitrary", "arbitrary")),
    )(flag, *operands)


def backward_kernel(flag_ref, *refs, causal, tiles, scale, waits):
    refs = refs[:7] + refs[7 + waits:]
    q_ref, k_ref, v_ref, g_ref, att_ref, m_ref, l_ref, dq_ref, dk_ref, dv_ref, dq_sc = refs
    tile = pl.program_id(1)

    @pl.when(tile == 0)
    def _():
        dq_sc[...] = jnp.zeros(dq_sc.shape, jnp.float32)

    @pl.when(flag_ref[0] == 1)
    def _():
        q = q_ref[...]
        k = k_ref[...]
        g = g_ref[...]
        scores = block_scores(q, k, tile, causal, scale)
        probs = jnp.exp(scores - m_ref[:, :1]) * (1.0 / l_ref[:, :1])
        weights = probs.astype(jnp.bfloat16)
        dots = lax.dot_general(g, v_ref[...], (((1,), (1,)), ((), ())), preferred_element_type=jnp.float32)
        delta = jnp.sum(g.astype(jnp.float32) * att_ref[...], axis=1, keepdims=True)
        slopes = (probs * (dots - delta) * scale).astype(jnp.bfloat16)
        dq_sc[...] += jnp.dot(slopes, k, preferred_element_type=jnp.float32)
        dk_ref[...] = lax.dot_general(slopes, q, (((0,), (0,)), ((), ())), preferred_element_type=jnp.float32)
        dv_ref[...] = lax.dot_general(weights, g, (((0,), (0,)), ((), ())), preferred_element_type=jnp.float32)

    @pl.when(flag_ref[0] != 1)
    def _():
        dk_ref[...] = jnp.zeros(dk_ref.shape, jnp.float32)
        dv_ref[...] = jnp.zeros(dv_ref.shape, jnp.float32)

    @pl.when(tile == tiles - 1)
    def _():
        dq_ref[...] = dq_sc[...]


def backward_block(flag, queries, keys, values, grads, attended32, row_max, row_total, causal, scale, after=()):
    block_len, cols = queries.shape
    heads = cols // DH
    tiles = block_len // KEY_TILE
    row_spec = pl.BlockSpec((block_len, DH), lambda h, t, f: (0, h))
    key_spec = pl.BlockSpec((KEY_TILE, DH), lambda h, t, f: (t, h))
    kernel = functools.partial(backward_kernel, causal=causal, tiles=tiles, scale=scale, waits=len(after))
    return pl.pallas_call(
        kernel,
        grid_spec=pltpu.PrefetchScalarGridSpec(
            num_scalar_prefetch=1,
            grid=(heads, tiles),
            in_specs=[row_spec, key_spec, key_spec, row_spec, row_spec, row_spec, row_spec]
            + [pl.BlockSpec(memory_space=pl.ANY)] * len(after),
            out_specs=[row_spec, key_spec, key_spec],
            scratch_shapes=[pltpu.VMEM((block_len, DH), jnp.float32)],
        ),
        out_shape=[jax.ShapeDtypeStruct((block_len, cols), jnp.float32)] * 3,
        compiler_params=pltpu.CompilerParams(dimension_semantics=("arbitrary", "arbitrary")),
    )(flag, queries, keys, values, grads, attended32, row_max, row_total, *after)


def local(queries, keys, values, out_weight, cotangent, block_keep):
    block_len = queries.shape[0]
    local_cols = queries.shape[1]
    score_scale = 1.0 / math.sqrt(DH)
    axis_len = lax.axis_size("ctx")
    levels = axis_len.bit_length() - 1
    block_index = lax.axis_index("ctx")
    stacked = jnp.stack([keys, values])
    remote = [passed_along(stacked, "ctx", 1 << level) for level in range(levels)]
    row_pick = lax.broadcasted_iota(jnp.int32, block_keep.shape, 0) == block_index
    keep_row = jnp.sum(jnp.where(row_pick, block_keep, 0), axis=0)
    column_ids = lax.broadcasted_iota(jnp.int32, keep_row.shape, 0)
    own_flag = jnp.ones((1,), jnp.int32)
    flags = []
    for level in range(levels):
        target = block_index - (1 << level)
        linked = jnp.sum(jnp.where(column_ids == target, keep_row, 0))
        flags.append(((target >= 0) & (linked == 1)).astype(jnp.int32).reshape(1))

    tp_len = lax.axis_size("tp")
    tp_index = lax.axis_index("tp")
    weight_cols = lax.all_to_all(out_weight, "tp", split_axis=1, concat_axis=0, tiled=True)
    grad_part = lax.dot_general(
        cotangent, weight_cols, (((1,), (1,)), ((), ())), preferred_element_type=jnp.float32
    )
    grad_parts = lax.all_to_all(
        grad_part.astype(jnp.bfloat16).reshape(block_len, tp_len, local_cols), "tp", 1, 1, tiled=True
    )
    grad_heads = jnp.sum(grad_parts.astype(jnp.float32), axis=1).astype(jnp.bfloat16)

    state = forward_block(own_flag, queries, keys, values, None, True, score_scale)
    for number, level in enumerate(FORWARD_ORDER[:levels]):
        after = (grad_heads,) if number == levels - 1 else ()
        state = forward_block(
            flags[level], queries, remote[level][0], remote[level][1], state, False, score_scale, after
        )
    row_max, row_total, total = state
    attended32 = total / row_total
    attended = attended32.astype(jnp.bfloat16)
    spread = jnp.broadcast_to(attended[None], (tp_len,) + attended.shape)
    att_parts = lax.all_to_all(spread, "tp", 0, 0, tiled=True)
    mixed_sum = jnp.einsum(
        "ktc,kcf->tf",
        att_parts,
        weight_cols.reshape(tp_len, local_cols, weight_cols.shape[1]),
        preferred_element_type=jnp.float32,
    )
    mixed = mixed_sum.astype(jnp.bfloat16)
    weight_part = jnp.einsum("ktc,tf->kcf", att_parts, cotangent, preferred_element_type=jnp.float32)
    halves = cotangent.shape[1] // local_cols
    pieces = (
        weight_part.astype(jnp.bfloat16)
        .reshape(tp_len, local_cols, halves, local_cols)
        .transpose(0, 2, 1, 3)
        .reshape(tp_len * halves, local_cols, local_cols)
    )
    reduced = jnp.sum(lax.all_to_all(pieces, "ctx", 0, 0, tiled=True).astype(jnp.float32), axis=0)
    moves = []
    for k in range(axis_len):
        for p in range(tp_len):
            moves.append((k * tp_len + p, (halves * p + k % halves) * tp_len + k // halves))
    d_weight = lax.ppermute(reduced.astype(jnp.bfloat16), ("ctx", "tp"), moves).astype(jnp.float32)
    arrived = []
    query_parts = []
    after = ()
    for level in BACKWARD_ORDER[:levels]:
        part, key_grad, value_grad = backward_block(
            flags[level], queries, remote[level][0], remote[level][1], grad_heads, attended32, row_max, row_total,
            False, score_scale, after,
        )
        query_parts.append(part)
        back = jnp.stack([key_grad, value_grad]).astype(jnp.bfloat16)
        arrived.append(passed_along(back, "ctx", -(1 << level)))
        after = (back,) + tuple(arrived[-3:-2])
    part, own_key, own_value = backward_block(
        own_flag, queries, keys, values, grad_heads, attended32, row_max, row_total, True, score_scale, after
    )
    arrived = [back.astype(jnp.float32) for back in arrived]
    grad_query = part
    for part in query_parts:
        grad_query = grad_query + part
    for back in arrived:
        own_key = own_key + back[0]
        own_value = own_value + back[1]
    return (mixed, grad_query, own_key, own_value, d_weight)


def solution(mesh):
    in_specs = (P("ctx", "tp"), P("ctx", "tp"), P("ctx", "tp"), P("tp", None), P("ctx", "tp"), P())
    out_specs = (P("ctx", "tp"), P("ctx", "tp"), P("ctx", "tp"), P("ctx", "tp"), P("tp", "ctx"))
    return jax.shard_map(local, mesh=mesh, in_specs=in_specs, out_specs=out_specs, check_vma=False)
```

```python
import functools
import math

import jax
import jax.numpy as jnp
from jax import lax
from jax.experimental import pallas as pl
from jax.experimental.pallas import tpu as pltpu
from jax.sharding import PartitionSpec as P

DH = 128
NEG = -1e30
KEY_TILE = 1024
FORWARD_ORDER = (0, 2, 1, 3)
BACKWARD_ORDER = (3, 1, 2, 0)


def passed_along(value, axis, steps):
    count = lax.axis_size(axis)
    initial, last = (max(0, -steps), min(count, count - steps))
    return lax.ppermute(value, axis, [(source, source + steps) for source in range(initial, last)])


def block_scores(q, k, tile, causal, scale):
    raw = lax.dot_general(q, k, (((1,), (1,)), ((), ())), preferred_element_type=jnp.float32) * scale
    if not causal:
        return raw
    rows = lax.broadcasted_iota(jnp.int32, raw.shape, 0)
    cols = lax.broadcasted_iota(jnp.int32, raw.shape, 1) + tile * raw.shape[1]
    return jnp.where(rows >= cols, raw, NEG)


def forward_kernel(flag_ref, *refs, causal, first, tiles, scale, waits, heads):
    refs = refs[:3] + refs[3 + waits:]
    if first:
        q_ref, k_ref, v_ref, m_ref, l_ref, acc_ref, m_sc, l_sc, acc_sc = refs
    else:
        q_ref, k_ref, v_ref, m_in, l_in, acc_in, m_ref, l_ref, acc_ref, m_sc, l_sc, acc_sc = refs
    tile = pl.program_id(1)
    for head in range(heads):
        cols = pl.ds(head * DH, DH)

        @pl.when(tile == 0)
        def _():
            if first:
                m_sc[head] = jnp.full(m_sc.shape[1:], NEG, jnp.float32)
                l_sc[head] = jnp.zeros(l_sc.shape[1:], jnp.float32)
                acc_sc[:, cols] = jnp.zeros((acc_sc.shape[0], DH), jnp.float32)
            else:
                m_sc[head] = m_in[:, pl.ds(head * DH, 1)]
                l_sc[head] = l_in[:, pl.ds(head * DH, 1)]
                acc_sc[:, cols] = acc_in[:, cols]

        @pl.when(flag_ref[0] == 1)
        def _():
            scores = block_scores(q_ref[:, cols], k_ref[:, cols], tile, causal, scale)
            old = m_sc[head]
            new = jnp.maximum(old, jnp.max(scores, axis=1, keepdims=True))
            alpha = jnp.exp(old - new)
            expd = jnp.exp(scores - new)
            l_sc[head] = l_sc[head] * alpha + jnp.sum(expd, axis=1, keepdims=True)
            acc_sc[:, cols] = acc_sc[:, cols] * alpha + jnp.dot(
                expd.astype(jnp.bfloat16), v_ref[:, cols], preferred_element_type=jnp.float32
            )
            m_sc[head] = new

        @pl.when(tile == tiles - 1)
        def _():
            m_ref[:, cols] = jnp.broadcast_to(m_sc[head], (m_ref.shape[0], DH))
            l_ref[:, cols] = jnp.broadcast_to(l_sc[head], (l_ref.shape[0], DH))
            acc_ref[:, cols] = acc_sc[:, cols]


def forward_block(flag, queries, keys, values, state, causal, scale, after=()):
    block_len, cols = queries.shape
    heads = cols // DH
    tiles = block_len // KEY_TILE
    first = state is None
    row_spec = pl.BlockSpec((block_len, cols), lambda h, t, f: (0, 0))
    key_spec = pl.BlockSpec((KEY_TILE, cols), lambda h, t, f: (t, 0))
    in_specs = [row_spec, key_spec, key_spec] + [pl.BlockSpec(memory_space=pl.ANY)] * len(after)
    operands = [queries, keys, values] + list(after)
    if not first:
        in_specs += [row_spec, row_spec, row_spec]
        operands += list(state)
    kernel = functools.partial(
        forward_kernel, causal=causal, first=first, tiles=tiles, scale=scale, waits=len(after), heads=heads
    )
    return pl.pallas_call(
        kernel,
        grid_spec=pltpu.PrefetchScalarGridSpec(
            num_scalar_prefetch=1,
            grid=(1, tiles),
            in_specs=in_specs,
            out_specs=[row_spec, row_spec, row_spec],
            scratch_shapes=[
                pltpu.VMEM((heads, block_len, 1), jnp.float32),
                pltpu.VMEM((heads, block_len, 1), jnp.float32),
                pltpu.VMEM((block_len, cols), jnp.float32),
            ],
        ),
        out_shape=[jax.ShapeDtypeStruct((block_len, cols), jnp.float32)] * 3,
        compiler_params=pltpu.CompilerParams(dimension_semantics=("arbitrary", "arbitrary")),
    )(flag, *operands)


def backward_kernel(flag_ref, *refs, causal, tiles, scale, waits):
    refs = refs[:7] + refs[7 + waits:]
    q_ref, k_ref, v_ref, g_ref, att_ref, m_ref, l_ref, dq_ref, dk_ref, dv_ref, dq_sc = refs
    tile = pl.program_id(1)

    @pl.when(tile == 0)
    def _():
        dq_sc[...] = jnp.zeros(dq_sc.shape, jnp.float32)

    @pl.when(flag_ref[0] == 1)
    def _():
        q = q_ref[...]
        k = k_ref[...]
        g = g_ref[...]
        scores = block_scores(q, k, tile, causal, scale)
        probs = jnp.exp(scores - m_ref[:, :1]) * (1.0 / l_ref[:, :1])
        weights = probs.astype(jnp.bfloat16)
        dots = lax.dot_general(g, v_ref[...], (((1,), (1,)), ((), ())), preferred_element_type=jnp.float32)
        delta = jnp.sum(g.astype(jnp.float32) * att_ref[...], axis=1, keepdims=True)
        slopes = (probs * (dots - delta) * scale).astype(jnp.bfloat16)
        dq_sc[...] += jnp.dot(slopes, k, preferred_element_type=jnp.float32)
        dk_ref[...] = lax.dot_general(slopes, q, (((0,), (0,)), ((), ())), preferred_element_type=jnp.float32)
        dv_ref[...] = lax.dot_general(weights, g, (((0,), (0,)), ((), ())), preferred_element_type=jnp.float32)

    @pl.when(flag_ref[0] != 1)
    def _():
        dk_ref[...] = jnp.zeros(dk_ref.shape, jnp.float32)
        dv_ref[...] = jnp.zeros(dv_ref.shape, jnp.float32)

    @pl.when(tile == tiles - 1)
    def _():
        dq_ref[...] = dq_sc[...]


def backward_block(flag, queries, keys, values, grads, attended32, row_max, row_total, causal, scale, after=()):
    block_len, cols = queries.shape
    heads = cols // DH
    tiles = block_len // KEY_TILE
    row_spec = pl.BlockSpec((block_len, DH), lambda h, t, f: (0, h))
    key_spec = pl.BlockSpec((KEY_TILE, DH), lambda h, t, f: (t, h))
    kernel = functools.partial(backward_kernel, causal=causal, tiles=tiles, scale=scale, waits=len(after))
    return pl.pallas_call(
        kernel,
        grid_spec=pltpu.PrefetchScalarGridSpec(
            num_scalar_prefetch=1,
            grid=(heads, tiles),
            in_specs=[row_spec, key_spec, key_spec, row_spec, row_spec, row_spec, row_spec]
            + [pl.BlockSpec(memory_space=pl.ANY)] * len(after),
            out_specs=[row_spec, key_spec, key_spec],
            scratch_shapes=[pltpu.VMEM((block_len, DH), jnp.float32)],
        ),
        out_shape=[jax.ShapeDtypeStruct((block_len, cols), jnp.float32)] * 3,
        compiler_params=pltpu.CompilerParams(dimension_semantics=("arbitrary", "arbitrary")),
    )(flag, queries, keys, values, grads, attended32, row_max, row_total, *after)


def local(queries, keys, values, out_weight, cotangent, block_keep):
    block_len = queries.shape[0]
    local_cols = queries.shape[1]
    score_scale = 1.0 / math.sqrt(DH)
    axis_len = lax.axis_size("ctx")
    levels = axis_len.bit_length() - 1
    block_index = lax.axis_index("ctx")
    stacked = jnp.stack([keys, values])
    remote = [passed_along(stacked, "ctx", 1 << level) for level in range(levels)]
    row_pick = lax.broadcasted_iota(jnp.int32, block_keep.shape, 0) == block_index
    keep_row = jnp.sum(jnp.where(row_pick, block_keep, 0), axis=0)
    column_ids = lax.broadcasted_iota(jnp.int32, keep_row.shape, 0)
    own_flag = jnp.ones((1,), jnp.int32)
    flags = []
    for level in range(levels):
        target = block_index - (1 << level)
        linked = jnp.sum(jnp.where(column_ids == target, keep_row, 0))
        flags.append(((target >= 0) & (linked == 1)).astype(jnp.int32).reshape(1))

    tp_len = lax.axis_size("tp")
    tp_index = lax.axis_index("tp")
    weight_cols = lax.all_to_all(out_weight, "tp", split_axis=1, concat_axis=0, tiled=True)
    grad_part = lax.dot_general(
        cotangent, weight_cols, (((1,), (1,)), ((), ())), preferred_element_type=jnp.float32
    )
    grad_parts = lax.all_to_all(
        grad_part.astype(jnp.bfloat16).reshape(block_len, tp_len, local_cols), "tp", 1, 1, tiled=True
    )
    grad_heads = jnp.sum(grad_parts.astype(jnp.float32), axis=1).astype(jnp.bfloat16)

    state = forward_block(own_flag, queries, keys, values, None, True, score_scale)
    for number, level in enumerate(FORWARD_ORDER[:levels]):
        after = (grad_heads,) if number == levels - 1 else ()
        state = forward_block(
            flags[level], queries, remote[level][0], remote[level][1], state, False, score_scale, after
        )
    row_max, row_total, total = state
    attended32 = total / row_total
    attended = attended32.astype(jnp.bfloat16)
    spread = jnp.broadcast_to(attended[None], (tp_len,) + attended.shape)
    att_parts = lax.all_to_all(spread, "tp", 0, 0, tiled=True)
    mixed_sum = jnp.einsum(
        "ktc,kcf->tf",
        att_parts,
        weight_cols.reshape(tp_len, local_cols, weight_cols.shape[1]),
        preferred_element_type=jnp.float32,
    )
    mixed = mixed_sum.astype(jnp.bfloat16)
    weight_part = jnp.einsum("ktc,tf->kcf", att_parts, cotangent, preferred_element_type=jnp.float32)
    halves = cotangent.shape[1] // local_cols
    pieces = (
        weight_part.astype(jnp.bfloat16)
        .reshape(tp_len, local_cols, halves, local_cols)
        .transpose(0, 2, 1, 3)
        .reshape(tp_len * halves, local_cols, local_cols)
    )
    reduced = jnp.sum(lax.all_to_all(pieces, "ctx", 0, 0, tiled=True).astype(jnp.float32), axis=0)
    moves = []
    for k in range(axis_len):
        for p in range(tp_len):
            moves.append((k * tp_len + p, (halves * p + k % halves) * tp_len + k // halves))
    d_weight = lax.ppermute(reduced.astype(jnp.bfloat16), ("ctx", "tp"), moves).astype(jnp.float32)
    arrived = []
    query_parts = []
    after = ()
    for level in BACKWARD_ORDER[:levels]:
        part, key_grad, value_grad = backward_block(
            flags[level], queries, remote[level][0], remote[level][1], grad_heads, attended32, row_max, row_total,
            False, score_scale, after,
        )
        query_parts.append(part)
        back = jnp.stack([key_grad, value_grad]).astype(jnp.bfloat16)
        arrived.append(passed_along(back, "ctx", -(1 << level)))
        after = (back,) + tuple(arrived[-3:-2])
    part, own_key, own_value = backward_block(
        own_flag, queries, keys, values, grad_heads, attended32, row_max, row_total, True, score_scale, after
    )
    arrived = [back.astype(jnp.float32) for back in arrived]
    grad_query = part
    for part in query_parts:
        grad_query = grad_query + part
    for back in arrived:
        own_key = own_key + back[0]
        own_value = own_value + back[1]
    return (mixed, grad_query, own_key, own_value, d_weight)


def solution(mesh):
    in_specs = (P("ctx", "tp"), P("ctx", "tp"), P("ctx", "tp"), P("tp", None), P("ctx", "tp"), P())
    out_specs = (P("ctx", "tp"), P("ctx", "tp"), P("ctx", "tp"), P("ctx", "tp"), P("tp", "ctx"))
    return jax.shard_map(local, mesh=mesh, in_specs=in_specs, out_specs=out_specs, check_vma=False)
```

```python
import functools
import math

import jax
import jax.numpy as jnp
from jax import lax
from jax.experimental import pallas as pl
from jax.experimental.pallas import tpu as pltpu
from jax.sharding import PartitionSpec as P

DH = 128
NEG = -1e30
KEY_TILE = 1024
BACKWARD_TILE = 512
FORWARD_ORDER = (0, 2, 1, 3)
BACKWARD_ORDER = (3, 1, 2, 0)


def passed_along(value, axis, steps):
    count = lax.axis_size(axis)
    initial, last = (max(0, -steps), min(count, count - steps))
    return lax.ppermute(value, axis, [(source, source + steps) for source in range(initial, last)])


def block_scores(q, k, tile, causal, scale):
    raw = lax.dot_general(q, k, (((1,), (1,)), ((), ())), preferred_element_type=jnp.float32) * scale
    if not causal:
        return raw
    rows = lax.broadcasted_iota(jnp.int32, raw.shape, 0)
    cols = lax.broadcasted_iota(jnp.int32, raw.shape, 1) + tile * raw.shape[1]
    return jnp.where(rows >= cols, raw, NEG)


def forward_kernel(flag_ref, *refs, causal, first, tiles, scale, waits):
    refs = refs[:3] + refs[3 + waits:]
    if first:
        q_ref, k_ref, v_ref, m_ref, l_ref, acc_ref, m_sc, l_sc, acc_sc = refs
    else:
        q_ref, k_ref, v_ref, m_in, l_in, acc_in, m_ref, l_ref, acc_ref, m_sc, l_sc, acc_sc = refs
    tile = pl.program_id(1)

    @pl.when(tile == 0)
    def _():
        if first:
            m_sc[...] = jnp.full(m_sc.shape, NEG, jnp.float32)
            l_sc[...] = jnp.zeros(l_sc.shape, jnp.float32)
            acc_sc[...] = jnp.zeros(acc_sc.shape, jnp.float32)
        else:
            m_sc[...] = m_in[:, :1]
            l_sc[...] = l_in[:, :1]
            acc_sc[...] = acc_in[...]

    @pl.when(flag_ref[0] == 1)
    def _():
        scores = block_scores(q_ref[...], k_ref[...], tile, causal, scale)
        old = m_sc[...]
        new = jnp.maximum(old, jnp.max(scores, axis=1, keepdims=True))
        alpha = jnp.exp(old - new)
        expd = jnp.exp(scores - new)
        l_sc[...] = l_sc[...] * alpha + jnp.sum(expd, axis=1, keepdims=True)
        acc_sc[...] = acc_sc[...] * alpha + jnp.dot(
            expd.astype(jnp.bfloat16), v_ref[...], preferred_element_type=jnp.float32
        )
        m_sc[...] = new

    @pl.when(tile == tiles - 1)
    def _():
        m_ref[...] = jnp.broadcast_to(m_sc[...], m_ref.shape)
        l_ref[...] = jnp.broadcast_to(l_sc[...], l_ref.shape)
        acc_ref[...] = acc_sc[...]


def forward_block(flag, queries, keys, values, state, causal, scale, after=()):
    block_len, cols = queries.shape
    heads = cols // DH
    tiles = block_len // KEY_TILE
    first = state is None
    row_spec = pl.BlockSpec((block_len, DH), lambda h, t, f: (0, h))
    key_spec = pl.BlockSpec((KEY_TILE, DH), lambda h, t, f: (t, h))
    in_specs = [row_spec, key_spec, key_spec] + [pl.BlockSpec(memory_space=pl.ANY)] * len(after)
    operands = [queries, keys, values] + list(after)
    if not first:
        in_specs += [row_spec, row_spec, row_spec]
        operands += list(state)
    kernel = functools.partial(
        forward_kernel, causal=causal, first=first, tiles=tiles, scale=scale, waits=len(after)
    )
    return pl.pallas_call(
        kernel,
        grid_spec=pltpu.PrefetchScalarGridSpec(
            num_scalar_prefetch=1,
            grid=(heads, tiles),
            in_specs=in_specs,
            out_specs=[row_spec, row_spec, row_spec],
            scratch_shapes=[
                pltpu.VMEM((block_len, 1), jnp.float32),
                pltpu.VMEM((block_len, 1), jnp.float32),
                pltpu.VMEM((block_len, DH), jnp.float32),
            ],
        ),
        out_shape=[jax.ShapeDtypeStruct((block_len, cols), jnp.float32)] * 3,
        compiler_params=pltpu.CompilerParams(dimension_semantics=("arbitrary", "arbitrary")),
    )(flag, *operands)


def backward_kernel(flag_ref, *refs, causal, tiles, scale, waits):
    refs = refs[:7] + refs[7 + waits:]
    q_ref, k_ref, v_ref, g_ref, att_ref, m_ref, l_ref, dq_ref, dk_ref, dv_ref, dq_sc = refs
    tile = pl.program_id(1)

    @pl.when(tile == 0)
    def _():
        dq_sc[...] = jnp.zeros(dq_sc.shape, jnp.float32)

    @pl.when(flag_ref[0] == 1)
    def _():
        q = q_ref[...]
        k = k_ref[...]
        g = g_ref[...]
        scores = block_scores(q, k, tile, causal, scale)
        probs = jnp.exp(scores - m_ref[:, :1]) * (1.0 / l_ref[:, :1])
        weights = probs.astype(jnp.bfloat16)
        dots = lax.dot_general(g, v_ref[...], (((1,), (1,)), ((), ())), preferred_element_type=jnp.float32)
        delta = jnp.sum(g.astype(jnp.float32) * att_ref[...], axis=1, keepdims=True)
        slopes = (probs * (dots - delta) * scale).astype(jnp.bfloat16)
        dq_sc[...] += jnp.dot(slopes, k, preferred_element_type=jnp.float32)
        dk_ref[...] = lax.dot_general(slopes, q, (((0,), (0,)), ((), ())), preferred_element_type=jnp.float32)
        dv_ref[...] = lax.dot_general(weights, g, (((0,), (0,)), ((), ())), preferred_element_type=jnp.float32)

    @pl.when(flag_ref[0] != 1)
    def _():
        dk_ref[...] = jnp.zeros(dk_ref.shape, jnp.float32)
        dv_ref[...] = jnp.zeros(dv_ref.shape, jnp.float32)

    @pl.when(tile == tiles - 1)
    def _():
        dq_ref[...] = dq_sc[...]


def backward_block(flag, queries, keys, values, grads, attended32, row_max, row_total, causal, scale, after=()):
    block_len, cols = queries.shape
    heads = cols // DH
    tiles = block_len // BACKWARD_TILE
    row_spec = pl.BlockSpec((block_len, DH), lambda h, t, f: (0, h))
    key_spec = pl.BlockSpec((BACKWARD_TILE, DH), lambda h, t, f: (t, h))
    kernel = functools.partial(backward_kernel, causal=causal, tiles=tiles, scale=scale, waits=len(after))
    return pl.pallas_call(
        kernel,
        grid_spec=pltpu.PrefetchScalarGridSpec(
            num_scalar_prefetch=1,
            grid=(heads, tiles),
            in_specs=[row_spec, key_spec, key_spec, row_spec, row_spec, row_spec, row_spec]
            + [pl.BlockSpec(memory_space=pl.ANY)] * len(after),
            out_specs=[row_spec, key_spec, key_spec],
            scratch_shapes=[pltpu.VMEM((block_len, DH), jnp.float32)],
        ),
        out_shape=[jax.ShapeDtypeStruct((block_len, cols), jnp.float32)] * 3,
        compiler_params=pltpu.CompilerParams(dimension_semantics=("arbitrary", "arbitrary")),
    )(flag, queries, keys, values, grads, attended32, row_max, row_total, *after)


def local(queries, keys, values, out_weight, cotangent, block_keep):
    block_len = queries.shape[0]
    local_cols = queries.shape[1]
    score_scale = 1.0 / math.sqrt(DH)
    axis_len = lax.axis_size("ctx")
    levels = axis_len.bit_length() - 1
    block_index = lax.axis_index("ctx")
    stacked = jnp.stack([keys, values])
    remote = [passed_along(stacked, "ctx", 1 << level) for level in range(levels)]
    row_pick = lax.broadcasted_iota(jnp.int32, block_keep.shape, 0) == block_index
    keep_row = jnp.sum(jnp.where(row_pick, block_keep, 0), axis=0)
    column_ids = lax.broadcasted_iota(jnp.int32, keep_row.shape, 0)
    own_flag = jnp.ones((1,), jnp.int32)
    flags = []
    for level in range(levels):
        target = block_index - (1 << level)
        linked = jnp.sum(jnp.where(column_ids == target, keep_row, 0))
        flags.append(((target >= 0) & (linked == 1)).astype(jnp.int32).reshape(1))

    tp_len = lax.axis_size("tp")
    tp_index = lax.axis_index("tp")
    weight_cols = lax.all_to_all(out_weight, "tp", split_axis=1, concat_axis=0, tiled=True)
    grad_part = lax.dot_general(
        cotangent, weight_cols, (((1,), (1,)), ((), ())), preferred_element_type=jnp.float32
    )
    grad_parts = lax.all_to_all(
        grad_part.astype(jnp.bfloat16).reshape(block_len, tp_len, local_cols), "tp", 1, 1, tiled=True
    )
    grad_heads = jnp.sum(grad_parts.astype(jnp.float32), axis=1).astype(jnp.bfloat16)

    state = forward_block(own_flag, queries, keys, values, None, True, score_scale)
    for number, level in enumerate(FORWARD_ORDER[:levels]):
        after = (grad_heads,) if number == levels - 1 else ()
        state = forward_block(
            flags[level], queries, remote[level][0], remote[level][1], state, False, score_scale, after
        )
    row_max, row_total, total = state
    attended32 = total / row_total
    attended = attended32.astype(jnp.bfloat16)
    spread = jnp.broadcast_to(attended[None], (tp_len,) + attended.shape)
    att_parts = lax.all_to_all(spread, "tp", 0, 0, tiled=True)
    mixed_sum = jnp.einsum(
        "ktc,kcf->tf",
        att_parts,
        weight_cols.reshape(tp_len, local_cols, weight_cols.shape[1]),
        preferred_element_type=jnp.float32,
    )
    mixed = mixed_sum.astype(jnp.bfloat16)
    weight_part = jnp.einsum("ktc,tf->kcf", att_parts, cotangent, preferred_element_type=jnp.float32)
    halves = cotangent.shape[1] // local_cols
    pieces = (
        weight_part.astype(jnp.bfloat16)
        .reshape(tp_len, local_cols, halves, local_cols)
        .transpose(0, 2, 1, 3)
        .reshape(tp_len * halves, local_cols, local_cols)
    )
    reduced = jnp.sum(lax.all_to_all(pieces, "ctx", 0, 0, tiled=True).astype(jnp.float32), axis=0)
    moves = []
    for k in range(axis_len):
        for p in range(tp_len):
            moves.append((k * tp_len + p, (halves * p + k % halves) * tp_len + k // halves))
    d_weight = lax.ppermute(reduced.astype(jnp.bfloat16), ("ctx", "tp"), moves).astype(jnp.float32)
    arrived = []
    query_parts = []
    after = ()
    for level in BACKWARD_ORDER[:levels]:
        part, key_grad, value_grad = backward_block(
            flags[level], queries, remote[level][0], remote[level][1], grad_heads, attended32, row_max, row_total,
            False, score_scale, after,
        )
        query_parts.append(part)
        back = jnp.stack([key_grad, value_grad]).astype(jnp.bfloat16)
        arrived.append(passed_along(back, "ctx", -(1 << level)))
        after = (back,) + tuple(arrived[-3:-2])
    part, own_key, own_value = backward_block(
        own_flag, queries, keys, values, grad_heads, attended32, row_max, row_total, True, score_scale, after
    )
    arrived = [back.astype(jnp.float32) for back in arrived]
    grad_query = part
    for part in query_parts:
        grad_query = grad_query + part
    for back in arrived:
        own_key = own_key + back[0]
        own_value = own_value + back[1]
    return (mixed, grad_query, own_key, own_value, d_weight)


def solution(mesh):
    in_specs = (P("ctx", "tp"), P("ctx", "tp"), P("ctx", "tp"), P("tp", None), P("ctx", "tp"), P())
    out_specs = (P("ctx", "tp"), P("ctx", "tp"), P("ctx", "tp"), P("ctx", "tp"), P("tp", "ctx"))
    return jax.shard_map(local, mesh=mesh, in_specs=in_specs, out_specs=out_specs, check_vma=False)
```
